32 devices in a mesh: aug: 4 (over x, core), dp: 8 (over z, y).
Axes of the slice: x: 2, y: 2, z: 4, core: 2. Of those that a mesh axis runs over, the one named last changes fastest.
Arguments:
- hidden: bfloat16 [4, 8, 128, 5120], P('aug', 'dp'), may hold values from -30 to 30, as said below
- output_grad: bfloat16 [4, 8, 128, 1280], P('aug', 'dp'), may hold values from -30 to 30, as said below
- down_weight: bfloat16 [5120, 1280], P('aug'), may hold values from -0.15625 to 0.15625
- first_moment: float32 [5120, 1280], P(('aug', 'dp')), may hold values from -6 to 6
- second_moment: float32 [5120, 1280], P(('aug', 'dp')), may hold values from 0.01 to 1
- noise: float32 [5120, 1280], P(('aug', 'dp')), may hold values from -6 to 6
Outputs:
- image_norms: float32 [8], P('dp')
- clipped_mean: float32 [5120, 1280], P(('aug', 'dp'))
- new_first: float32 [5120, 1280], P(('aug', 'dp'))
- new_second: float32 [5120, 1280], P(('aug', 'dp'))
- update: float32 [5120, 1280], P(('aug', 'dp'))
- hidden_grad: bfloat16 [4, 8, 128, 5120], P(None, 'dp', None, 'aug')
The draws below stay inside these ranges and needn't reach their ends.
Inputs may be any that keep to these rules, and one draw needn't show every extreme that they name: `hidden`: finite activations of every view. `output_grad`: finite output gradients of every view.
All inputs are finite; a program needn't handle non-finite values.
Results may differ from the reference program's by a relative error of at most 0.0004.
Values may be sent and summed in bfloat16 or wider, within the bound.
No kernel may reach another device: no remote copies, remote signals or barrier semaphores. Data moves between devices by JAX's collectives and lax.ppermute only.
A program may use at most 64 MiB of HBM per device.

```python
import math
import jax
import jax.numpy as jnp
from jax import lax

D = 1280
FF = 5120
PATCHES = 128
VIEWS = 4
IMAGES = 8


def scale_table(key, count):
    return jnp.exp(jax.random.uniform(key, (count,), jnp.float32, math.log(0.3), math.log(3.0)))


def column_ramp(count):
    return jnp.sqrt(1.0 + 2.0 * jnp.arange(count, dtype=jnp.float32) / count)


def draw_hidden(key, part):
    shape = (VIEWS, IMAGES, PATCHES, FF)
    columns = scale_table(jax.random.fold_in(key, 11), FF) * column_ramp(FF)
    values = jnp.clip(jax.random.normal(jax.random.fold_in(key, 14), shape, jnp.float32), -5.0, 5.0) * columns
    return values.astype(jnp.bfloat16)


def draw_output_grad(key, part):
    shape = (VIEWS, IMAGES, PATCHES, D)
    columns = scale_table(jax.random.fold_in(key, 21), D)
    images = scale_table(jax.random.fold_in(key, 22), IMAGES)
    scales = images[None, :, None, None] * columns[None, None, None, :]
    values = jnp.clip(jax.random.normal(jax.random.fold_in(key, 25), shape, jnp.float32), -3.0, 3.0) * scales
    return values.astype(jnp.bfloat16)


def levels(rng, shape, split, least, largest):
    def one(dim, blocks):
        draws = jax.random.uniform(jax.random.fold_in(jax.random.fold_in(rng, 6), dim), (blocks,), jnp.float32, least / len(split), largest / len(split))
        return jnp.repeat(jnp.exp(draws), shape[dim] // blocks).reshape((-1,) + (1,) * (len(shape) - dim - 1))

    loudness = one(*split[0])
    for cut in split[1:]:
        loudness = loudness * one(*cut)
    return loudness


def gaussian(own_key, extent, width, most, pieces=(), kind=jnp.bfloat16):
    gain = levels(own_key, extent, pieces, -0.22, 0.18) if pieces else 1.0
    result = jax.random.normal(own_key, extent, jnp.float32) * width * gain
    return jnp.minimum(jnp.maximum(result, -most), most).astype(kind)


def setup_inputs(seed: int = 0) -> dict:
    seeds = jax.random.split(jax.random.key(seed), 7)
    return {
        "hidden": draw_hidden(jax.random.fold_in(seeds[6], 71), 0),
        "output_grad": draw_output_grad(jax.random.fold_in(seeds[6], 71), 0),
        "down_weight": gaussian(seeds[2], (FF, D), D ** -0.5, 0.15625, ((0, 4),)),
        "first_moment": gaussian(seeds[3], (FF, D), 1.0, 6.0, ((0, 32),), jnp.float32),
        "second_moment": jnp.clip(jnp.exp(math.log(1.0) - 4.6051702 * jax.random.uniform(seeds[4], (FF, D), jnp.float32) ** levels(seeds[4], (FF, D), ((0, 32),), -0.2, 0.2)), 0.01, 1.0),
        "noise": gaussian(seeds[5], (FF, D), 1.0, 6.0, ((0, 32),), jnp.float32),
    }


clip_ratio = 1.9
noise_ratio = 0.002
beta_one = 0.9
beta_two = 0.999
adam_step = 10
adam_eps = 1e-08

def reference(hidden, output_grad, down_weight, first_moment, second_moment, noise):
    views = hidden.shape[0]
    clip = clip_ratio * math.sqrt(PATCHES * FF * D / VIEWS)

    def one_image(total, index):
        rows_h = lax.dynamic_index_in_dim(hidden, index, 1, keepdims=False).reshape(views * PATCHES, FF)
        rows_g = lax.dynamic_index_in_dim(output_grad, index, 1, keepdims=False).reshape(views * PATCHES, D)
        grad = jnp.dot(rows_h.T, rows_g, preferred_element_type=jnp.float32) / views
        norm = jnp.sqrt(jnp.sum(grad * grad))
        factor = clip / jnp.maximum(norm, clip)
        return (total + factor * grad, norm)
    total, image_norms = lax.scan(one_image, jnp.zeros((FF, D), jnp.float32), jnp.arange(IMAGES, dtype=jnp.int32))
    clipped_mean = total / IMAGES
    noisy = clipped_mean + noise_ratio * clip * noise / IMAGES
    new_first = beta_one * first_moment + (1.0 - beta_one) * noisy
    new_second = beta_two * second_moment + (1.0 - beta_two) * noisy * noisy
    update = new_first / (1.0 - beta_one ** adam_step) / (jnp.sqrt(new_second / (1.0 - beta_two ** adam_step)) + adam_eps)

    def one_view(grads):
        rows = grads.reshape(IMAGES * PATCHES, D)
        back = lax.dot_general(rows, down_weight, (((1,), (1,)), ((), ())), preferred_element_type=jnp.float32)
        return back.astype(jnp.bfloat16).reshape(IMAGES, PATCHES, FF)
    hidden_grad = lax.map(one_view, output_grad)
    return (image_norms, clipped_mean, new_first, new_second, update, hidden_grad)
```

```python
import math

import jax
import jax.numpy as jnp
from jax import lax
from jax.sharding import PartitionSpec as P

clip_ratio = 1.9
noise_ratio = 0.002
beta_one = 0.9
beta_two = 0.999
adam_step = 10
adam_eps = 1e-08


def project_back(rows, down_weight):
    return lax.dot_general(
        rows, down_weight, (((1,), (1,)), ((), ())), preferred_element_type=jnp.float32
    )


def grid_cycle(points):
    zs = sorted({z for z, _ in points})
    ys = sorted({y for _, y in points})
    if len(zs) * len(ys) != len(points):
        return None
    swap = len(zs) % 2 == 1
    if swap:
        zs, ys = ys, zs
    rows, cols = len(zs), len(ys)
    if rows % 2 == 1 or cols < 2:
        return None
    walk = [(0, c) for c in range(cols)]
    for r in range(1, rows):
        order = range(cols - 1, 0, -1) if r % 2 == 1 else range(1, cols)
        walk += [(r, c) for c in order]
    walk += [(r, 0) for r in range(rows - 1, 0, -1)]
    cycle = [(zs[r], ys[c]) for r, c in walk]
    if swap:
        cycle = [(y, z) for z, y in cycle]
    return cycle


def ring_order(mesh):
    column = list(mesh.devices[0, :])
    n = len(column)
    try:
        places = [(int(d.coords[2]), int(d.coords[1])) for d in column]
    except Exception:
        return list(range(n))
    cycle = grid_cycle(places)
    if cycle is None or len(set(places)) != n:
        return list(range(n))
    return [places.index(p) for p in cycle]


def ring_reduce_scatter(parts, ring, step_fn):
    n = len(ring)
    pos_of = [0] * n
    for k, d in enumerate(ring):
        pos_of[d] = k
    ring_arr = jnp.array(ring, jnp.int32)
    me = lax.axis_index("dp")
    pos = jnp.array(pos_of, jnp.int32)[me]
    right = [(ring[k], ring[(k + 1) % n]) for k in range(n)]
    left = [(ring[k], ring[(k - 1) % n]) for k in range(n)]
    acc_r = None
    acc_l = None
    for s in range(n - 1):
        blk_r = ring_arr[(pos - 1 - s) % n]
        blk_l = ring_arr[(pos + 1 + s) % n]
        own_r = parts(blk_r)[0]
        own_l = parts(blk_l)[1]
        send_r = own_r if acc_r is None else acc_r + own_r
        send_l = own_l if acc_l is None else acc_l + own_l
        acc_r = lax.ppermute(send_r, "dp", right)
        acc_l = lax.ppermute(send_l, "dp", left)
    mine = parts(me)
    return jnp.concatenate([acc_r + mine[0], acc_l + mine[1]], axis=0)


def per_device(ring, hidden, output_grad, down_weight, first_moment, second_moment, noise):
    views = lax.axis_size("aug")
    groups = lax.axis_size("dp")
    images_here = hidden.shape[1]
    patches = hidden.shape[2]
    width = hidden.shape[3]
    model_width = output_grad.shape[3]
    images_all = images_here * groups
    clip = clip_ratio * math.sqrt(patches * width * model_width / views)
    local_rows = images_here * patches
    swapped = lax.all_to_all(
        hidden.reshape(local_rows, width), "aug", split_axis=1, concat_axis=0, tiled=True
    )
    slice_width = swapped.shape[1]
    grad_rows = output_grad.reshape(local_rows, model_width)
    every = lax.all_gather(grad_rows, "aug", axis=0, tiled=True)
    h_four = swapped.reshape(views, images_here, patches, slice_width)
    g_four = every.reshape(views, images_here, patches, model_width)
    summed = jnp.einsum("vipf,vipd->ifd", h_four, g_four, preferred_element_type=jnp.float32)
    back_rows = project_back(every, down_weight)
    hidden_grad = back_rows.astype(jnp.bfloat16).reshape(views, images_here, patches, slice_width)
    grads = summed / views
    partial_value = jnp.sum(grads * grads, axis=(1, 2))
    squares = lax.psum(partial_value, "aug")
    image_norms = jnp.sqrt(squares)
    factor = clip / jnp.maximum(image_norms, clip)
    owned_rows = slice_width // groups
    half = owned_rows // 2

    def parts(block):
        start = block * owned_rows
        rows = lax.dynamic_slice_in_dim(grads, start, owned_rows, axis=1)
        clipped = jnp.sum(factor[:, None, None] * rows, axis=0)
        return clipped[:half], clipped[half:]

    owned = ring_reduce_scatter(parts, ring, None)
    clipped_mean = owned / images_all
    noisy = clipped_mean + noise_ratio * clip * noise / images_all
    new_first = beta_one * first_moment + (1.0 - beta_one) * noisy
    new_second = beta_two * second_moment + (1.0 - beta_two) * noisy * noisy
    update = (
        new_first
        / (1.0 - beta_one**adam_step)
        / (jnp.sqrt(new_second / (1.0 - beta_two**adam_step)) + adam_eps)
    )
    return (image_norms, clipped_mean, new_first, new_second, update, hidden_grad)


def solution(mesh):
    in_specs = (
        P("aug", "dp", None, None),
        P("aug", "dp", None, None),
        P("aug", None),
        P(("aug", "dp"), None),
        P(("aug", "dp"), None),
        P(("aug", "dp"), None),
    )
    out_specs = (
        P("dp"),
        P(("aug", "dp"), None),
        P(("aug", "dp"), None),
        P(("aug", "dp"), None),
        P(("aug", "dp"), None),
        P(None, "dp", None, "aug"),
    )
    ring = ring_order(mesh)

    def body(*args):
        return per_device(ring, *args)

    return jax.shard_map(
        body, mesh=mesh, in_specs=in_specs, out_specs=out_specs, check_vma=False
    )
```

```python
import math

import jax
import jax.numpy as jnp
from jax import lax
from jax.sharding import PartitionSpec as P

clip_ratio = 1.9
noise_ratio = 0.002
beta_one = 0.9
beta_two = 0.999
adam_step = 10
adam_eps = 1e-08


def project_back(rows, down_weight):
    return lax.dot_general(
        rows, down_weight, (((1,), (1,)), ((), ())), preferred_element_type=jnp.float32
    )


def grid_cycle(points):
    zs = sorted({z for z, _ in points})
    ys = sorted({y for _, y in points})
    if len(zs) * len(ys) != len(points):
        return None
    swap = len(zs) % 2 == 1
    if swap:
        zs, ys = ys, zs
    rows, cols = len(zs), len(ys)
    if rows % 2 == 1 or cols < 2:
        return None
    walk = [(0, c) for c in range(cols)]
    for r in range(1, rows):
        order = range(cols - 1, 0, -1) if r % 2 == 1 else range(1, cols)
        walk += [(r, c) for c in order]
    walk += [(r, 0) for r in range(rows - 1, 0, -1)]
    cycle = [(zs[r], ys[c]) for r, c in walk]
    if swap:
        cycle = [(y, z) for z, y in cycle]
    return cycle


def ring_order(mesh):
    column = list(mesh.devices[0, :])
    n = len(column)
    try:
        places = [(int(d.coords[2]), int(d.coords[1])) for d in column]
    except Exception:
        return list(range(n))
    cycle = grid_cycle(places)
    if cycle is None or len(set(places)) != n:
        return list(range(n))
    return [places.index(p) for p in cycle]


def ring_reduce_scatter(parts, ring, step_fn):
    n = len(ring)
    pos_of = [0] * n
    for k, d in enumerate(ring):
        pos_of[d] = k
    ring_arr = jnp.array(ring, jnp.int32)
    me = lax.axis_index("dp")
    pos = jnp.array(pos_of, jnp.int32)[me]
    right = [(ring[k], ring[(k + 1) % n]) for k in range(n)]
    left = [(ring[k], ring[(k - 1) % n]) for k in range(n)]
    acc_r = None
    acc_l = None
    for s in range(n - 1):
        blk_r = ring_arr[(pos - 1 - s) % n]
        blk_l = ring_arr[(pos + 1 + s) % n]
        if acc_r is None:
            send_r = parts(blk_r, 0, None)
            send_l = parts(blk_l, 1, None)
        else:
            send_r = acc_r + parts(blk_r, 0, acc_r)
            send_l = acc_l + parts(blk_l, 1, acc_l)
        acc_r = lax.ppermute(send_r, "dp", right)
        acc_l = lax.ppermute(send_l, "dp", left)
    return jnp.concatenate(
        [acc_r + parts(me, 0, acc_r), acc_l + parts(me, 1, acc_l)], axis=0
    )


def exchange_four(h_rows, grad_rows):
    a = lax.axis_index("aug")
    rows = h_rows.shape[0]
    sw = h_rows.shape[1] // 4

    def cols(b):
        return lax.dynamic_slice_in_dim(h_rows, b * sw, sw, axis=1)

    over_x = [(i, i ^ 2) for i in range(4)]
    over_core = [(i, i ^ 1) for i in range(4)]
    far = lax.ppermute(
        jnp.concatenate([cols(a ^ 2), cols(a ^ 3), grad_rows], axis=1), "aug", over_x
    )
    near = lax.ppermute(cols(a ^ 1), "aug", over_core)
    far_mine = far[:, :sw]
    relay = lax.ppermute(
        jnp.concatenate([far[:, sw:2 * sw], far[:, 2 * sw:], grad_rows], axis=1),
        "aug",
        over_core,
    )
    d = grad_rows.shape[1]
    h_from = {0: cols(a), 1: near, 2: far_mine, 3: relay[:, :sw]}
    g_from = {0: grad_rows, 1: relay[:, sw + d:], 2: far[:, 2 * sw:], 3: relay[:, sw:sw + d]}
    h_all = jnp.zeros((4 * rows, sw), h_rows.dtype)
    g_all = jnp.zeros((4 * rows, grad_rows.shape[1]), grad_rows.dtype)
    for m in range(4):
        at = (a ^ m) * rows
        h_all = lax.dynamic_update_slice_in_dim(h_all, h_from[m], at, axis=0)
        g_all = lax.dynamic_update_slice_in_dim(g_all, g_from[m], at, axis=0)
    return h_all, g_all


def butterfly_sum(value, n):
    if n & (n - 1):
        return lax.psum(value, "aug")
    bit = 1
    while bit < n:
        value = value + lax.ppermute(value, "aug", [(i, i ^ bit) for i in range(n)])
        bit *= 2
    return value


def per_device(ring, hidden, output_grad, down_weight, first_moment, second_moment, noise):
    views = lax.axis_size("aug")
    groups = lax.axis_size("dp")
    images_here = hidden.shape[1]
    patches = hidden.shape[2]
    width = hidden.shape[3]
    model_width = output_grad.shape[3]
    images_all = images_here * groups
    clip = clip_ratio * math.sqrt(patches * width * model_width / views)
    local_rows = images_here * patches
    h_rows = hidden.reshape(local_rows, width)
    grad_rows = output_grad.reshape(local_rows, model_width)
    if views == 4:
        swapped, every = exchange_four(h_rows, grad_rows)
    else:
        swapped = lax.all_to_all(h_rows, "aug", split_axis=1, concat_axis=0, tiled=True)
        every = lax.all_gather(grad_rows, "aug", axis=0, tiled=True)
    slice_width = swapped.shape[1]
    h_four = swapped.reshape(views, images_here, patches, slice_width)
    g_four = every.reshape(views, images_here, patches, model_width)
    summed = jnp.einsum("vipf,vipd->ifd", h_four, g_four, preferred_element_type=jnp.float32)
    back_rows = project_back(every, down_weight)
    hidden_grad = back_rows.astype(jnp.bfloat16).reshape(views, images_here, patches, slice_width)
    grads = summed / views
    partial_value = jnp.sum(grads * grads, axis=(1, 2))
    squares = butterfly_sum(partial_value, views)
    image_norms = jnp.sqrt(squares)
    factor = clip / jnp.maximum(image_norms, clip)
    owned_rows = slice_width // groups
    half = owned_rows // 2

    def parts(block, which, after):
        source = grads
        if after is not None:
            _, source = lax.optimization_barrier((after, grads))
        start = block * owned_rows + which * half
        rows = lax.dynamic_slice_in_dim(source, start, half, axis=1)
        return jnp.sum(factor[:, None, None] * rows, axis=0)

    owned = ring_reduce_scatter(parts, ring, None)
    clipped_mean = owned / images_all
    noisy = clipped_mean + noise_ratio * clip * noise / images_all
    new_first = beta_one * first_moment + (1.0 - beta_one) * noisy
    new_second = beta_two * second_moment + (1.0 - beta_two) * noisy * noisy
    update = (
        new_first
        / (1.0 - beta_one**adam_step)
        / (jnp.sqrt(new_second / (1.0 - beta_two**adam_step)) + adam_eps)
    )
    return (image_norms, clipped_mean, new_first, new_second, update, hidden_grad)


def solution(mesh):
    in_specs = (
        P("aug", "dp", None, None),
        P("aug", "dp", None, None),
        P("aug", None),
        P(("aug", "dp"), None),
        P(("aug", "dp"), None),
        P(("aug", "dp"), None),
    )
    out_specs = (
        P("dp"),
        P(("aug", "dp"), None),
        P(("aug", "dp"), None),
        P(("aug", "dp"), None),
        P(("aug", "dp"), None),
        P(None, "dp", None, "aug"),
    )
    ring = ring_order(mesh)

    def body(*args):
        return per_device(ring, *args)

    return jax.shard_map(
        body, mesh=mesh, in_specs=in_specs, out_specs=out_specs, check_vma=False
    )
```

```python
import math

import jax
import jax.numpy as jnp
from jax import lax
from jax.sharding import PartitionSpec as P

clip_ratio = 1.9
noise_ratio = 0.002
beta_one = 0.9
beta_two = 0.999
adam_step = 10
adam_eps = 1e-08


def project_back(rows, down_weight):
    return lax.dot_general(
        rows, down_weight, (((1,), (1,)), ((), ())), preferred_element_type=jnp.float32
    )


def grid_cycle(points):
    zs = sorted({z for z, _ in points})
    ys = sorted({y for _, y in points})
    if len(zs) * len(ys) != len(points):
        return None
    swap = len(zs) % 2 == 1
    if swap:
        zs, ys = ys, zs
    rows, cols = len(zs), len(ys)
    if rows % 2 == 1 or cols < 2:
        return None
    walk = [(0, c) for c in range(cols)]
    for r in range(1, rows):
        order = range(cols - 1, 0, -1) if r % 2 == 1 else range(1, cols)
        walk += [(r, c) for c in order]
    walk += [(r, 0) for r in range(rows - 1, 0, -1)]
    cycle = [(zs[r], ys[c]) for r, c in walk]
    if swap:
        cycle = [(y, z) for z, y in cycle]
    return cycle


def ring_order(mesh):
    column = list(mesh.devices[0, :])
    n = len(column)
    try:
        places = [(int(d.coords[2]), int(d.coords[1])) for d in column]
    except Exception:
        return list(range(n))
    cycle = grid_cycle(places)
    if cycle is None or len(set(places)) != n:
        return list(range(n))
    return [places.index(p) for p in cycle]


def ring_reduce_scatter(parts, ring, step_fn):
    n = len(ring)
    pos_of = [0] * n
    for k, d in enumerate(ring):
        pos_of[d] = k
    ring_arr = jnp.array(ring, jnp.int32)
    me = lax.axis_index("dp")
    pos = jnp.array(pos_of, jnp.int32)[me]
    right = [(ring[k], ring[(k + 1) % n]) for k in range(n)]
    left = [(ring[k], ring[(k - 1) % n]) for k in range(n)]
    def block(s, step):
        return ring_arr[(pos - 1 - s) % n] if step < 0 else ring_arr[(pos + 1 + s) % n]

    own_r = parts(block(0, -1), 0, None)
    own_l = parts(block(0, 1), 1, None)
    acc_r = None
    acc_l = None
    for s in range(n - 1):
        send_r = own_r if acc_r is None else acc_r + own_r
        send_l = own_l if acc_l is None else acc_l + own_l
        acc_r = lax.ppermute(send_r, "dp", right)
        acc_l = lax.ppermute(send_l, "dp", left)
        own_r = parts(block(s + 1, -1), 0, send_r)
        own_l = parts(block(s + 1, 1), 1, send_l)
    return jnp.concatenate([acc_r + own_r, acc_l + own_l], axis=0)


def exchange_four(h_rows, grad_rows):
    a = lax.axis_index("aug")
    rows = h_rows.shape[0]
    sw = h_rows.shape[1] // 4
    d = grad_rows.shape[1]

    def cols(b):
        return lax.dynamic_slice_in_dim(h_rows, b * sw, sw, axis=1)

    over_x = [(i, i ^ 2) for i in range(4)]
    over_core = [(i, i ^ 1) for i in range(4)]
    far = lax.ppermute(
        jnp.concatenate([cols(a ^ 2), cols(a ^ 3), grad_rows], axis=1), "aug", over_x
    )
    near = lax.ppermute(jnp.concatenate([cols(a ^ 1), grad_rows], axis=1), "aug", over_core)
    relay = lax.ppermute(far[:, sw:], "aug", over_core)
    return [
        (a * rows, cols(a), grad_rows),
        ((a ^ 1) * rows, near[:, :sw], near[:, sw:]),
        ((a ^ 2) * rows, far[:, :sw], far[:, 2 * sw:]),
        ((a ^ 3) * rows, relay[:, :sw], relay[:, sw:]),
    ]


def butterfly_sum(value, n):
    if n & (n - 1):
        return lax.psum(value, "aug")
    bit = 1
    while bit < n:
        value = value + lax.ppermute(value, "aug", [(i, i ^ bit) for i in range(n)])
        bit *= 2
    return value


def per_device(ring, hidden, output_grad, down_weight, first_moment, second_moment, noise):
    views = lax.axis_size("aug")
    groups = lax.axis_size("dp")
    images_here = hidden.shape[1]
    patches = hidden.shape[2]
    width = hidden.shape[3]
    model_width = output_grad.shape[3]
    images_all = images_here * groups
    clip = clip_ratio * math.sqrt(patches * width * model_width / views)
    local_rows = images_here * patches
    h_rows = hidden.reshape(local_rows, width)
    grad_rows = output_grad.reshape(local_rows, model_width)
    if views == 4 and images_here == 1:
        pieces = exchange_four(h_rows, grad_rows)
        slice_width = pieces[0][1].shape[1]
        summed = None
        hidden_grad = jnp.zeros((views * local_rows, slice_width), jnp.bfloat16)
        for at, h_piece, g_piece in pieces:
            term = jnp.dot(h_piece.T, g_piece, preferred_element_type=jnp.float32)
            summed = term if summed is None else summed + term
            back = project_back(g_piece, down_weight).astype(jnp.bfloat16)
            hidden_grad = lax.dynamic_update_slice_in_dim(hidden_grad, back, at, axis=0)
        summed = summed[None]
        hidden_grad = hidden_grad.reshape(views, images_here, patches, slice_width)
    else:
        swapped = lax.all_to_all(h_rows, "aug", split_axis=1, concat_axis=0, tiled=True)
        every = lax.all_gather(grad_rows, "aug", axis=0, tiled=True)
        slice_width = swapped.shape[1]
        h_four = swapped.reshape(views, images_here, patches, slice_width)
        g_four = every.reshape(views, images_here, patches, model_width)
        summed = jnp.einsum("vipf,vipd->ifd", h_four, g_four, preferred_element_type=jnp.float32)
        back_rows = project_back(every, down_weight)
        hidden_grad = back_rows.astype(jnp.bfloat16).reshape(views, images_here, patches, slice_width)
    grads = summed / views
    partial_value = jnp.sum(grads * grads, axis=(1, 2))
    squares = butterfly_sum(partial_value, views)
    image_norms = jnp.sqrt(squares)
    factor = clip / jnp.maximum(image_norms, clip)
    owned_rows = slice_width // groups
    half = owned_rows // 2

    def parts(block, which, after):
        source = grads
        if after is not None:
            _, source = lax.optimization_barrier((after, grads))
        start = block * owned_rows + which * half
        rows = lax.dynamic_slice_in_dim(source, start, half, axis=1)
        return lax.optimization_barrier(jnp.sum(factor[:, None, None] * rows, axis=0))

    owned = ring_reduce_scatter(parts, ring, None)
    clipped_mean = owned / images_all
    noisy = clipped_mean + noise_ratio * clip * noise / images_all
    new_first = beta_one * first_moment + (1.0 - beta_one) * noisy
    new_second = beta_two * second_moment + (1.0 - beta_two) * noisy * noisy
    update = (
        new_first
        / (1.0 - beta_one**adam_step)
        / (jnp.sqrt(new_second / (1.0 - beta_two**adam_step)) + adam_eps)
    )
    return (image_norms, clipped_mean, new_first, new_second, update, hidden_grad)


def solution(mesh):
    in_specs = (
        P("aug", "dp", None, None),
        P("aug", "dp", None, None),
        P("aug", None),
        P(("aug", "dp"), None),
        P(("aug", "dp"), None),
        P(("aug", "dp"), None),
    )
    out_specs = (
        P("dp"),
        P(("aug", "dp"), None),
        P(("aug", "dp"), None),
        P(("aug", "dp"), None),
        P(("aug", "dp"), None),
        P(None, "dp", None, "aug"),
    )
    ring = ring_order(mesh)

    def body(*args):
        return per_device(ring, *args)

    return jax.shard_map(
        body, mesh=mesh, in_specs=in_specs, out_specs=out_specs, check_vma=False
    )
```

```python
import math

import jax
import jax.numpy as jnp
from jax import lax
from jax.sharding import PartitionSpec as P

clip_ratio = 1.9
noise_ratio = 0.002
beta_one = 0.9
beta_two = 0.999
adam_step = 10
adam_eps = 1e-08


def project_back(rows, down_weight):
    return lax.dot_general(
        rows, down_weight, (((1,), (1,)), ((), ())), preferred_element_type=jnp.float32
    )


def grid_cycle(points):
    zs = sorted({z for z, _ in points})
    ys = sorted({y for _, y in points})
    if len(zs) * len(ys) != len(points):
        return None
    swap = len(zs) % 2 == 1
    if swap:
        zs, ys = ys, zs
    rows, cols = len(zs), len(ys)
    if rows % 2 == 1 or cols < 2:
        return None
    walk = [(0, c) for c in range(cols)]
    for r in range(1, rows):
        order = range(cols - 1, 0, -1) if r % 2 == 1 else range(1, cols)
        walk += [(r, c) for c in order]
    walk += [(r, 0) for r in range(rows - 1, 0, -1)]
    cycle = [(zs[r], ys[c]) for r, c in walk]
    if swap:
        cycle = [(y, z) for z, y in cycle]
    return cycle


def ring_order(mesh):
    column = list(mesh.devices[0, :])
    n = len(column)
    try:
        places = [(int(d.coords[2]), int(d.coords[1])) for d in column]
    except Exception:
        return list(range(n))
    cycle = grid_cycle(places)
    if cycle is None or len(set(places)) != n:
        return list(range(n))
    return [places.index(p) for p in cycle]


def lookup(table, index):
    out = jnp.int32(table[0])
    for k in range(1, len(table)):
        out = jnp.where(index == k, jnp.int32(table[k]), out)
    return out


def ring_reduce_scatter(parts, ring, step_fn):
    n = len(ring)
    pos_of = [0] * n
    for k, d in enumerate(ring):
        pos_of[d] = k
    me = lax.axis_index("dp")
    pos = lookup(pos_of, me)
    right = [(ring[k], ring[(k + 1) % n]) for k in range(n)]
    left = [(ring[k], ring[(k - 1) % n]) for k in range(n)]
    def block(s, step):
        return lookup(ring, (pos - 1 - s) % n if step < 0 else (pos + 1 + s) % n)

    own_r = parts(block(0, -1), 0, None)
    own_l = parts(block(0, 1), 1, None)
    acc_r = None
    acc_l = None
    for s in range(n - 1):
        send_r = own_r if acc_r is None else acc_r + own_r
        send_l = own_l if acc_l is None else acc_l + own_l
        acc_r = lax.ppermute(send_r, "dp", right)
        acc_l = lax.ppermute(send_l, "dp", left)
        own_r = parts(block(s + 1, -1), 0, send_r)
        own_l = parts(block(s + 1, 1), 1, send_l)
    return jnp.concatenate([acc_r + own_r, acc_l + own_l], axis=0)


def exchange_four(h_rows, grad_rows):
    a = lax.axis_index("aug")
    rows = h_rows.shape[0]
    sw = h_rows.shape[1] // 4
    d = grad_rows.shape[1]

    def cols(b):
        return lax.dynamic_slice_in_dim(h_rows, b * sw, sw, axis=1)

    over_x = [(i, i ^ 2) for i in range(4)]
    over_core = [(i, i ^ 1) for i in range(4)]
    far_first = lax.ppermute(
        jnp.concatenate([cols(a ^ 3), grad_rows], axis=1), "aug", over_x
    )
    near = lax.ppermute(jnp.concatenate([cols(a ^ 1), grad_rows], axis=1), "aug", over_core)
    _, second = lax.optimization_barrier((far_first, cols(a ^ 2)))
    far_second = lax.ppermute(second, "aug", over_x)
    relay = lax.ppermute(far_first, "aug", over_core)
    return [
        (a * rows, cols(a), grad_rows),
        ((a ^ 1) * rows, near[:, :sw], near[:, sw:]),
        ((a ^ 2) * rows, far_second, far_first[:, sw:]),
        ((a ^ 3) * rows, relay[:, :sw], relay[:, sw:]),
    ]


def butterfly_sum(value, n):
    if n == 4:
        a = lax.axis_index("aug")
        got = {0: value}
        for m in (1, 2, 3):
            got[m] = lax.ppermute(value, "aug", [(i, i ^ m) for i in range(4)])
        total = None
        for k in range(4):
            term = got[3]
            for m in (2, 1, 0):
                term = jnp.where((a ^ m) == k, got[m], term)
            total = term if total is None else total + term
        return total
    if n & (n - 1):
        return lax.psum(value, "aug")
    bit = 1
    while bit < n:
        value = value + lax.ppermute(value, "aug", [(i, i ^ bit) for i in range(n)])
        bit *= 2
    return value


def per_device(ring, hidden, output_grad, down_weight, first_moment, second_moment, noise):
    views = lax.axis_size("aug")
    groups = lax.axis_size("dp")
    images_here = hidden.shape[1]
    patches = hidden.shape[2]
    width = hidden.shape[3]
    model_width = output_grad.shape[3]
    images_all = images_here * groups
    clip = clip_ratio * math.sqrt(patches * width * model_width / views)
    local_rows = images_here * patches
    h_rows = hidden.reshape(local_rows, width)
    grad_rows = output_grad.reshape(local_rows, model_width)
    if views == 4 and images_here == 1:
        pieces = exchange_four(h_rows, grad_rows)
        slice_width = pieces[0][1].shape[1]
        summed = None
        hidden_grad = jnp.zeros((views * local_rows, slice_width), jnp.bfloat16)
        for at, h_piece, g_piece in pieces:
            term = jnp.dot(h_piece.T, g_piece, preferred_element_type=jnp.float32)
            summed = term if summed is None else summed + term
            back = project_back(g_piece, down_weight).astype(jnp.bfloat16)
            hidden_grad = lax.dynamic_update_slice_in_dim(hidden_grad, back, at, axis=0)
        summed = summed[None]
        hidden_grad = hidden_grad.reshape(views, images_here, patches, slice_width)
    else:
        swapped = lax.all_to_all(h_rows, "aug", split_axis=1, concat_axis=0, tiled=True)
        every = lax.all_gather(grad_rows, "aug", axis=0, tiled=True)
        slice_width = swapped.shape[1]
        h_four = swapped.reshape(views, images_here, patches, slice_width)
        g_four = every.reshape(views, images_here, patches, model_width)
        summed = jnp.einsum("vipf,vipd->ifd", h_four, g_four, preferred_element_type=jnp.float32)
        back_rows = project_back(every, down_weight)
        hidden_grad = back_rows.astype(jnp.bfloat16).reshape(views, images_here, patches, slice_width)
    grads = summed / views
    partial_value = jnp.sum(grads * grads, axis=(1, 2))
    squares = butterfly_sum(partial_value, views)
    image_norms = jnp.sqrt(squares)
    factor = clip / jnp.maximum(image_norms, clip)
    owned_rows = slice_width // groups
    half = owned_rows // 2

    def parts(block, which, after):
        source = grads
        if after is not None:
            _, source = lax.optimization_barrier((after, grads))
        start = block * owned_rows + which * half
        rows = lax.dynamic_slice_in_dim(source, start, half, axis=1)
        return lax.optimization_barrier(jnp.sum(factor[:, None, None] * rows, axis=0))

    owned = ring_reduce_scatter(parts, ring, None)
    clipped_mean = owned / images_all
    noisy = clipped_mean + noise_ratio * clip * noise / images_all
    new_first = beta_one * first_moment + (1.0 - beta_one) * noisy
    new_second = beta_two * second_moment + (1.0 - beta_two) * noisy * noisy
    update = (
        new_first
        / (1.0 - beta_one**adam_step)
        / (jnp.sqrt(new_second / (1.0 - beta_two**adam_step)) + adam_eps)
    )
    return (image_norms, clipped_mean, new_first, new_second, update, hidden_grad)


def solution(mesh):
    in_specs = (
        P("aug", "dp", None, None),
        P("aug", "dp", None, None),
        P("aug", None),
        P(("aug", "dp"), None),
        P(("aug", "dp"), None),
        P(("aug", "dp"), None),
    )
    out_specs = (
        P("dp"),
        P(("aug", "dp"), None),
        P(("aug", "dp"), None),
        P(("aug", "dp"), None),
        P(("aug", "dp"), None),
        P(None, "dp", None, "aug"),
    )
    ring = ring_order(mesh)

    def body(*args):
        return per_device(ring, *args)

    return jax.shard_map(
        body, mesh=mesh, in_specs=in_specs, out_specs=out_specs, check_vma=False
    )
```

```python
import math

import jax
import jax.numpy as jnp
from jax import lax
from jax.sharding import PartitionSpec as P

clip_ratio = 1.9
noise_ratio = 0.002
beta_one = 0.9
beta_two = 0.999
adam_step = 10
adam_eps = 1e-08


def project_back(rows, down_weight):
    return lax.dot_general(
        rows, down_weight, (((1,), (1,)), ((), ())), preferred_element_type=jnp.float32
    )


def grid_cycle(points):
    zs = sorted({z for z, _ in points})
    ys = sorted({y for _, y in points})
    if len(zs) * len(ys) != len(points):
        return None
    swap = len(zs) % 2 == 1
    if swap:
        zs, ys = ys, zs
    rows, cols = len(zs), len(ys)
    if rows % 2 == 1 or cols < 2:
        return None
    walk = [(0, c) for c in range(cols)]
    for r in range(1, rows):
        order = range(cols - 1, 0, -1) if r % 2 == 1 else range(1, cols)
        walk += [(r, c) for c in order]
    walk += [(r, 0) for r in range(rows - 1, 0, -1)]
    cycle = [(zs[r], ys[c]) for r, c in walk]
    if swap:
        cycle = [(y, z) for z, y in cycle]
    return cycle


def ring_order(mesh):
    column = list(mesh.devices[0, :])
    n = len(column)
    try:
        places = [(int(d.coords[2]), int(d.coords[1])) for d in column]
    except Exception:
        return list(range(n))
    cycle = grid_cycle(places)
    if cycle is None or len(set(places)) != n:
        return list(range(n))
    return [places.index(p) for p in cycle]


def lookup(table, index):
    out = jnp.int32(table[0])
    for k in range(1, len(table)):
        out = jnp.where(index == k, jnp.int32(table[k]), out)
    return out


def ring_reduce_scatter(parts, ring, step_fn):
    n = len(ring)
    pos_of = [0] * n
    for k, d in enumerate(ring):
        pos_of[d] = k
    me = lax.axis_index("dp")
    pos = lookup(pos_of, me)
    right = [(ring[k], ring[(k + 1) % n]) for k in range(n)]
    left = [(ring[k], ring[(k - 1) % n]) for k in range(n)]
    def block(s, step):
        return lookup(ring, (pos - 1 - s) % n if step < 0 else (pos + 1 + s) % n)

    own_r = parts(block(0, -1), 0, None)
    own_l = parts(block(0, 1), 1, None)
    acc_r = None
    acc_l = None
    for s in range(n - 1):
        send_r = own_r if acc_r is None else acc_r + own_r
        send_l = own_l if acc_l is None else acc_l + own_l
        acc_r = lax.ppermute(send_r, "dp", right)
        acc_l = lax.ppermute(send_l, "dp", left)
        own_r = parts(block(s + 1, -1), 0, send_r)
        own_l = parts(block(s + 1, 1), 1, send_l)
    return jnp.concatenate([acc_r + own_r, acc_l + own_l], axis=0)


def exchange_four(h_rows, grad_rows):
    a = lax.axis_index("aug")
    rows = h_rows.shape[0]
    sw = h_rows.shape[1] // 4
    d = grad_rows.shape[1]

    def cols(b):
        return lax.dynamic_slice_in_dim(h_rows, b * sw, sw, axis=1)

    over_x = [(i, i ^ 2) for i in range(4)]
    over_core = [(i, i ^ 1) for i in range(4)]
    far_first = lax.ppermute(
        jnp.concatenate([cols(a ^ 3), grad_rows], axis=1), "aug", over_x
    )
    near = lax.ppermute(jnp.concatenate([cols(a ^ 1), grad_rows], axis=1), "aug", over_core)
    _, second = lax.optimization_barrier((far_first, cols(a ^ 2)))
    far_second = lax.ppermute(second, "aug", over_x)
    relay = lax.ppermute(far_first, "aug", over_core)
    return [
        (a * rows, cols(a), grad_rows),
        ((a ^ 1) * rows, near[:, :sw], near[:, sw:]),
        ((a ^ 2) * rows, far_second, far_first[:, sw:]),
        ((a ^ 3) * rows, relay[:, :sw], relay[:, sw:]),
    ]


def butterfly_sum(value, n):
    if n == 4:
        got = {}
        for m in (1, 2, 3):
            got[m] = lax.ppermute(value, "aug", [(i, i ^ m) for i in range(4)])
        return (value + got[1]) + (got[2] + got[3])
    if n & (n - 1):
        return lax.psum(value, "aug")
    bit = 1
    while bit < n:
        value = value + lax.ppermute(value, "aug", [(i, i ^ bit) for i in range(n)])
        bit *= 2
    return value


def per_device(ring, hidden, output_grad, down_weight, first_moment, second_moment, noise):
    views = lax.axis_size("aug")
    groups = lax.axis_size("dp")
    images_here = hidden.shape[1]
    patches = hidden.shape[2]
    width = hidden.shape[3]
    model_width = output_grad.shape[3]
    images_all = images_here * groups
    clip = clip_ratio * math.sqrt(patches * width * model_width / views)
    local_rows = images_here * patches
    h_rows = hidden.reshape(local_rows, width)
    grad_rows = output_grad.reshape(local_rows, model_width)
    if views == 4 and images_here == 1:
        pieces = exchange_four(h_rows, grad_rows)
        slice_width = pieces[0][1].shape[1]
        summed = None
        hidden_grad = jnp.zeros((views * local_rows, slice_width), jnp.bfloat16)
        for at, h_piece, g_piece in pieces:
            term = jnp.dot(h_piece.T, g_piece, preferred_element_type=jnp.float32)
            summed = term if summed is None else summed + term
            back = project_back(g_piece, down_weight).astype(jnp.bfloat16)
            hidden_grad = lax.dynamic_update_slice_in_dim(hidden_grad, back, at, axis=0)
        summed = summed[None]
        hidden_grad = hidden_grad.reshape(views, images_here, patches, slice_width)
    else:
        swapped = lax.all_to_all(h_rows, "aug", split_axis=1, concat_axis=0, tiled=True)
        every = lax.all_gather(grad_rows, "aug", axis=0, tiled=True)
        slice_width = swapped.shape[1]
        h_four = swapped.reshape(views, images_here, patches, slice_width)
        g_four = every.reshape(views, images_here, patches, model_width)
        summed = jnp.einsum("vipf,vipd->ifd", h_four, g_four, preferred_element_type=jnp.float32)
        back_rows = project_back(every, down_weight)
        hidden_grad = back_rows.astype(jnp.bfloat16).reshape(views, images_here, patches, slice_width)
    grads = summed / views
    partial_value = jnp.sum(grads * grads, axis=(1, 2))
    squares = butterfly_sum(partial_value, views)
    image_norms = jnp.sqrt(squares)
    factor = clip / jnp.maximum(image_norms, clip)
    owned_rows = slice_width // groups
    half = owned_rows // 2

    def parts(block, which, after):
        source = grads
        if after is not None:
            _, source = lax.optimization_barrier((after, grads))
        start = block * owned_rows + which * half
        rows = lax.dynamic_slice_in_dim(source, start, half, axis=1)
        return lax.optimization_barrier(jnp.sum(factor[:, None, None] * rows, axis=0))

    owned = ring_reduce_scatter(parts, ring, None)
    clipped_mean = owned / images_all
    noisy = clipped_mean + noise_ratio * clip * noise / images_all
    new_first = beta_one * first_moment + (1.0 - beta_one) * noisy
    new_second = beta_two * second_moment + (1.0 - beta_two) * noisy * noisy
    update = (
        new_first
        / (1.0 - beta_one**adam_step)
        / (jnp.sqrt(new_second / (1.0 - beta_two**adam_step)) + adam_eps)
    )
    return (image_norms, clipped_mean, new_first, new_second, update, hidden_grad)


def solution(mesh):
    in_specs = (
        P("aug", "dp", None, None),
        P("aug", "dp", None, None),
        P("aug", None),
        P(("aug", "dp"), None),
        P(("aug", "dp"), None),
        P(("aug", "dp"), None),
    )
    out_specs = (
        P("dp"),
        P(("aug", "dp"), None),
        P(("aug", "dp"), None),
        P(("aug", "dp"), None),
        P(("aug", "dp"), None),
        P(None, "dp", None, "aug"),
    )
    ring = ring_order(mesh)

    def body(*args):
        return per_device(ring, *args)

    return jax.shard_map(
        body, mesh=mesh, in_specs=in_specs, out_specs=out_specs, check_vma=False
    )
```

```python
import math

import jax
import jax.numpy as jnp
from jax import lax
from jax.sharding import PartitionSpec as P

clip_ratio = 1.9
noise_ratio = 0.002
beta_one = 0.9
beta_two = 0.999
adam_step = 10
adam_eps = 1e-08


def project_back(rows, down_weight):
    return lax.dot_general(
        rows, down_weight, (((1,), (1,)), ((), ())), preferred_element_type=jnp.float32
    )


def grid_cycle(points):
    zs = sorted({z for z, _ in points})
    ys = sorted({y for _, y in points})
    if len(zs) * len(ys) != len(points):
        return None
    swap = len(zs) % 2 == 1
    if swap:
        zs, ys = ys, zs
    rows, cols = len(zs), len(ys)
    if rows % 2 == 1 or cols < 2:
        return None
    walk = [(0, c) for c in range(cols)]
    for r in range(1, rows):
        order = range(cols - 1, 0, -1) if r % 2 == 1 else range(1, cols)
        walk += [(r, c) for c in order]
    walk += [(r, 0) for r in range(rows - 1, 0, -1)]
    cycle = [(zs[r], ys[c]) for r, c in walk]
    if swap:
        cycle = [(y, z) for z, y in cycle]
    return cycle


def ring_order(mesh):
    column = list(mesh.devices[0, :])
    n = len(column)
    try:
        places = [(int(d.coords[2]), int(d.coords[1])) for d in column]
    except Exception:
        return list(range(n))
    cycle = grid_cycle(places)
    if cycle is None or len(set(places)) != n:
        return list(range(n))
    return [places.index(p) for p in cycle]


def lookup(table, index):
    out = jnp.int32(table[0])
    for k in range(1, len(table)):
        out = jnp.where(index == k, jnp.int32(table[k]), out)
    return out


def ring_reduce_scatter(parts, ring, pieces):
    n = len(ring)
    pos_of = [0] * n
    for k, d in enumerate(ring):
        pos_of[d] = k
    me = lax.axis_index("dp")
    pos = lookup(pos_of, me)
    right = [(ring[k], ring[(k + 1) % n]) for k in range(n)]
    left = [(ring[k], ring[(k - 1) % n]) for k in range(n)]
    def block(s, step):
        return lookup(ring, (pos - 1 - s) % n if step < 0 else (pos + 1 + s) % n)

    chains = [(-1 if c % 2 == 0 else 1, c) for c in range(pieces)]
    own = [parts(block(0, step), which, None) for step, which in chains]
    acc = [None] * pieces
    for s in range(n - 1):
        send = [o if x is None else x + o for x, o in zip(acc, own)]
        acc = [
            lax.ppermute(v, "dp", right if step < 0 else left)
            for v, (step, _) in zip(send, chains)
        ]
        own = [
            parts(block(s + 1, step), which, v)
            for v, (step, which) in zip(send, chains)
        ]
    return jnp.concatenate([x + o for x, o in zip(acc, own)], axis=0)


def exchange_four(h_rows, grad_rows):
    a = lax.axis_index("aug")
    rows = h_rows.shape[0]
    sw = h_rows.shape[1] // 4
    d = grad_rows.shape[1]

    def cols(b):
        return lax.dynamic_slice_in_dim(h_rows, b * sw, sw, axis=1)

    over_x = [(i, i ^ 2) for i in range(4)]
    over_core = [(i, i ^ 1) for i in range(4)]
    far_first = lax.ppermute(
        jnp.concatenate([cols(a ^ 3), grad_rows], axis=1), "aug", over_x
    )
    near = lax.ppermute(jnp.concatenate([cols(a ^ 1), grad_rows], axis=1), "aug", over_core)
    _, second = lax.optimization_barrier((far_first, cols(a ^ 2)))
    far_second = lax.ppermute(second, "aug", over_x)
    relay = lax.ppermute(far_first, "aug", over_core)
    return [
        (a * rows, cols(a), grad_rows),
        ((a ^ 1) * rows, near[:, :sw], near[:, sw:]),
        ((a ^ 2) * rows, far_second, far_first[:, sw:]),
        ((a ^ 3) * rows, relay[:, :sw], relay[:, sw:]),
    ]


def butterfly_sum(value, n):
    if n == 4:
        got = {}
        for m in (1, 2, 3):
            got[m] = lax.ppermute(value, "aug", [(i, i ^ m) for i in range(4)])
        return (value + got[1]) + (got[2] + got[3])
    if n & (n - 1):
        return lax.psum(value, "aug")
    bit = 1
    while bit < n:
        value = value + lax.ppermute(value, "aug", [(i, i ^ bit) for i in range(n)])
        bit *= 2
    return value


def per_device(ring, hidden, output_grad, down_weight, first_moment, second_moment, noise):
    views = lax.axis_size("aug")
    groups = lax.axis_size("dp")
    images_here = hidden.shape[1]
    patches = hidden.shape[2]
    width = hidden.shape[3]
    model_width = output_grad.shape[3]
    images_all = images_here * groups
    clip = clip_ratio * math.sqrt(patches * width * model_width / views)
    local_rows = images_here * patches
    h_rows = hidden.reshape(local_rows, width)
    grad_rows = output_grad.reshape(local_rows, model_width)
    if views == 4 and images_here == 1:
        pieces = exchange_four(h_rows, grad_rows)
        slice_width = pieces[0][1].shape[1]
        summed = None
        hidden_grad = jnp.zeros((views * local_rows, slice_width), jnp.bfloat16)
        for at, h_piece, g_piece in pieces:
            term = jnp.dot(h_piece.T, g_piece, preferred_element_type=jnp.float32)
            summed = term if summed is None else summed + term
            back = project_back(g_piece, down_weight).astype(jnp.bfloat16)
            hidden_grad = lax.dynamic_update_slice_in_dim(hidden_grad, back, at, axis=0)
        summed = summed[None]
        hidden_grad = hidden_grad.reshape(views, images_here, patches, slice_width)
    else:
        swapped = lax.all_to_all(h_rows, "aug", split_axis=1, concat_axis=0, tiled=True)
        every = lax.all_gather(grad_rows, "aug", axis=0, tiled=True)
        slice_width = swapped.shape[1]
        h_four = swapped.reshape(views, images_here, patches, slice_width)
        g_four = every.reshape(views, images_here, patches, model_width)
        summed = jnp.einsum("vipf,vipd->ifd", h_four, g_four, preferred_element_type=jnp.float32)
        back_rows = project_back(every, down_weight)
        hidden_grad = back_rows.astype(jnp.bfloat16).reshape(views, images_here, patches, slice_width)
    grads = summed / views
    partial_value = jnp.sum(grads * grads, axis=(1, 2))
    squares = butterfly_sum(partial_value, views)
    image_norms = jnp.sqrt(squares)
    factor = clip / jnp.maximum(image_norms, clip)
    owned_rows = slice_width // groups
    pieces = 4 if owned_rows % 32 == 0 else 2
    half = owned_rows // pieces

    def parts(block, which, after):
        source = grads
        if after is not None:
            _, source = lax.optimization_barrier((after, grads))
        start = block * owned_rows + which * half
        rows = lax.dynamic_slice_in_dim(source, start, half, axis=1)
        return lax.optimization_barrier(jnp.sum(factor[:, None, None] * rows, axis=0))

    owned = ring_reduce_scatter(parts, ring, pieces)
    clipped_mean = owned / images_all
    noisy = clipped_mean + noise_ratio * clip * noise / images_all
    new_first = beta_one * first_moment + (1.0 - beta_one) * noisy
    new_second = beta_two * second_moment + (1.0 - beta_two) * noisy * noisy
    update = (
        new_first
        / (1.0 - beta_one**adam_step)
        / (jnp.sqrt(new_second / (1.0 - beta_two**adam_step)) + adam_eps)
    )
    return (image_norms, clipped_mean, new_first, new_second, update, hidden_grad)


def solution(mesh):
    in_specs = (
        P("aug", "dp", None, None),
        P("aug", "dp", None, None),
        P("aug", None),
        P(("aug", "dp"), None),
        P(("aug", "dp"), None),
        P(("aug", "dp"), None),
    )
    out_specs = (
        P("dp"),
        P(("aug", "dp"), None),
        P(("aug", "dp"), None),
        P(("aug", "dp"), None),
        P(("aug", "dp"), None),
        P(None, "dp", None, "aug"),
    )
    ring = ring_order(mesh)

    def body(*args):
        return per_device(ring, *args)

    return jax.shard_map(
        body, mesh=mesh, in_specs=in_specs, out_specs=out_specs, check_vma=False
    )
```

```python
import math

import jax
import jax.numpy as jnp
from jax import lax
from jax.sharding import PartitionSpec as P

clip_ratio = 1.9
noise_ratio = 0.002
beta_one = 0.9
beta_two = 0.999
adam_step = 10
adam_eps = 1e-08


def project_back(rows, down_weight):
    return lax.dot_general(
        rows, down_weight, (((1,), (1,)), ((), ())), preferred_element_type=jnp.float32
    )


def grid_cycle(points):
    zs = sorted({z for z, _ in points})
    ys = sorted({y for _, y in points})
    if len(zs) * len(ys) != len(points):
        return None
    swap = len(zs) % 2 == 1
    if swap:
        zs, ys = ys, zs
    rows, cols = len(zs), len(ys)
    if rows % 2 == 1 or cols < 2:
        return None
    walk = [(0, c) for c in range(cols)]
    for r in range(1, rows):
        order = range(cols - 1, 0, -1) if r % 2 == 1 else range(1, cols)
        walk += [(r, c) for c in order]
    walk += [(r, 0) for r in range(rows - 1, 0, -1)]
    cycle = [(zs[r], ys[c]) for r, c in walk]
    if swap:
        cycle = [(y, z) for z, y in cycle]
    return cycle


def ring_order(mesh):
    column = list(mesh.devices[0, :])
    n = len(column)
    try:
        places = [(int(d.coords[2]), int(d.coords[1])) for d in column]
    except Exception:
        return list(range(n))
    cycle = grid_cycle(places)
    if cycle is None or len(set(places)) != n:
        return list(range(n))
    return [places.index(p) for p in cycle]


def lookup(table, index):
    out = jnp.int32(table[0])
    for k in range(1, len(table)):
        out = jnp.where(index == k, jnp.int32(table[k]), out)
    return out


def ring_reduce_scatter(rows_of, factor, ring, pieces):
    n = len(ring)
    pos_of = [0] * n
    for k, d in enumerate(ring):
        pos_of[d] = k
    me = lax.axis_index("dp")
    pos = lookup(pos_of, me)
    right = [(ring[k], ring[(k + 1) % n]) for k in range(n)]
    left = [(ring[k], ring[(k - 1) % n]) for k in range(n)]
    from_prev = lax.ppermute(factor, "dp", right)
    from_next = lax.ppermute(factor, "dp", left)

    def block(s, step):
        return lookup(ring, (pos - 1 - s) % n if step < 0 else (pos + 1 + s) % n)

    def scaled(s, step, which, after):
        rows = rows_of(block(s, step), which, after)
        return lax.optimization_barrier(factor * rows)

    chains = [(-1 if c % 2 == 0 else 1, c) for c in range(pieces)]
    own = [rows_of(block(0, step), which, None) for step, which in chains]
    acc = [None] * pieces
    unscaled = True
    for s in range(n - 1):
        if s == 0:
            send = own
        elif unscaled:
            send = [
                x * (from_prev if step < 0 else from_next) + o
                for x, o, (step, _) in zip(acc, own, chains)
            ]
            unscaled = False
        else:
            send = [x + o for x, o in zip(acc, own)]
        acc = [
            lax.ppermute(v, "dp", right if step < 0 else left)
            for v, (step, _) in zip(send, chains)
        ]
        own = [
            scaled(s + 1, step, which, v) for v, (step, which) in zip(send, chains)
        ]
    if unscaled:
        acc = [
            x * (from_prev if step < 0 else from_next) for x, (step, _) in zip(acc, chains)
        ]
    return jnp.concatenate([x + o for x, o in zip(acc, own)], axis=0)


def exchange_four(h_rows, grad_rows):
    a = lax.axis_index("aug")
    rows = h_rows.shape[0]
    sw = h_rows.shape[1] // 4
    d = grad_rows.shape[1]

    def cols(b):
        return lax.dynamic_slice_in_dim(h_rows, b * sw, sw, axis=1)

    over_x = [(i, i ^ 2) for i in range(4)]
    over_core = [(i, i ^ 1) for i in range(4)]
    far_first = lax.ppermute(
        jnp.concatenate([cols(a ^ 3), grad_rows], axis=1), "aug", over_x
    )
    near = lax.ppermute(jnp.concatenate([cols(a ^ 1), grad_rows], axis=1), "aug", over_core)
    _, second = lax.optimization_barrier((far_first, cols(a ^ 2)))
    far_second = lax.ppermute(second, "aug", over_x)
    relay = lax.ppermute(far_first, "aug", over_core)
    return [
        (a * rows, cols(a), grad_rows),
        ((a ^ 1) * rows, near[:, :sw], near[:, sw:]),
        ((a ^ 2) * rows, far_second, far_first[:, sw:]),
        ((a ^ 3) * rows, relay[:, :sw], relay[:, sw:]),
    ]


def butterfly_sum(value, n):
    if n == 4:
        got = {}
        for m in (1, 2, 3):
            got[m] = lax.ppermute(value, "aug", [(i, i ^ m) for i in range(4)])
        return (value + got[1]) + (got[2] + got[3])
    if n & (n - 1):
        return lax.psum(value, "aug")
    bit = 1
    while bit < n:
        value = value + lax.ppermute(value, "aug", [(i, i ^ bit) for i in range(n)])
        bit *= 2
    return value


def per_device(ring, hidden, output_grad, down_weight, first_moment, second_moment, noise):
    views = lax.axis_size("aug")
    groups = lax.axis_size("dp")
    images_here = hidden.shape[1]
    patches = hidden.shape[2]
    width = hidden.shape[3]
    model_width = output_grad.shape[3]
    images_all = images_here * groups
    clip = clip_ratio * math.sqrt(patches * width * model_width / views)
    local_rows = images_here * patches
    h_rows = hidden.reshape(local_rows, width)
    grad_rows = output_grad.reshape(local_rows, model_width)
    if views == 4 and images_here == 1:
        pieces = exchange_four(h_rows, grad_rows)
        slice_width = pieces[0][1].shape[1]
        summed = None
        hidden_grad = jnp.zeros((views * local_rows, slice_width), jnp.bfloat16)
        for at, h_piece, g_piece in pieces:
            term = jnp.dot(h_piece.T, g_piece, preferred_element_type=jnp.float32)
            summed = term if summed is None else summed + term
            back = project_back(g_piece, down_weight).astype(jnp.bfloat16)
            hidden_grad = lax.dynamic_update_slice_in_dim(hidden_grad, back, at, axis=0)
        summed = summed[None]
        hidden_grad = hidden_grad.reshape(views, images_here, patches, slice_width)
    else:
        swapped = lax.all_to_all(h_rows, "aug", split_axis=1, concat_axis=0, tiled=True)
        every = lax.all_gather(grad_rows, "aug", axis=0, tiled=True)
        slice_width = swapped.shape[1]
        h_four = swapped.reshape(views, images_here, patches, slice_width)
        g_four = every.reshape(views, images_here, patches, model_width)
        summed = jnp.einsum("vipf,vipd->ifd", h_four, g_four, preferred_element_type=jnp.float32)
        back_rows = project_back(every, down_weight)
        hidden_grad = back_rows.astype(jnp.bfloat16).reshape(views, images_here, patches, slice_width)
    grads = summed / views
    partial_value = jnp.sum(grads * grads, axis=(1, 2))
    squares = butterfly_sum(partial_value, views)
    image_norms = jnp.sqrt(squares)
    factor = clip / jnp.maximum(image_norms, clip)
    owned_rows = slice_width // groups
    pieces = 4 if owned_rows % 32 == 0 else 2
    half = owned_rows // pieces

    if images_here == 1:
        ring_rows, ring_factor = grads[0], factor[0]
    else:
        ring_rows = jnp.sum(factor[:, None, None] * grads, axis=0)
        ring_factor = jnp.float32(1.0)

    def rows_of(block, which, after):
        source = ring_rows
        if after is not None:
            _, source = lax.optimization_barrier((after, source))
        start = block * owned_rows + which * half
        return lax.dynamic_slice_in_dim(source, start, half, axis=0)

    owned = ring_reduce_scatter(rows_of, ring_factor, ring, pieces)
    clipped_mean = owned / images_all
    noisy = clipped_mean + noise_ratio * clip * noise / images_all
    new_first = beta_one * first_moment + (1.0 - beta_one) * noisy
    new_second = beta_two * second_moment + (1.0 - beta_two) * noisy * noisy
    update = (
        new_first
        / (1.0 - beta_one**adam_step)
        / (jnp.sqrt(new_second / (1.0 - beta_two**adam_step)) + adam_eps)
    )
    return (image_norms, clipped_mean, new_first, new_second, update, hidden_grad)


def solution(mesh):
    in_specs = (
        P("aug", "dp", None, None),
        P("aug", "dp", None, None),
        P("aug", None),
        P(("aug", "dp"), None),
        P(("aug", "dp"), None),
        P(("aug", "dp"), None),
    )
    out_specs = (
        P("dp"),
        P(("aug", "dp"), None),
        P(("aug", "dp"), None),
        P(("aug", "dp"), None),
        P(("aug", "dp"), None),
        P(None, "dp", None, "aug"),
    )
    ring = ring_order(mesh)

    def body(*args):
        return per_device(ring, *args)

    return jax.shard_map(
        body, mesh=mesh, in_specs=in_specs, out_specs=out_specs, check_vma=False
    )
```

```python
import math

import jax
import jax.numpy as jnp
from jax import lax
from jax.sharding import PartitionSpec as P

clip_ratio = 1.9
noise_ratio = 0.002
beta_one = 0.9
beta_two = 0.999
adam_step = 10
adam_eps = 1e-08


def project_back(rows, down_weight):
    return lax.dot_general(
        rows, down_weight, (((1,), (1,)), ((), ())), preferred_element_type=jnp.float32
    )


def grid_cycle(points):
    zs = sorted({z for z, _ in points})
    ys = sorted({y for _, y in points})
    if len(zs) * len(ys) != len(points):
        return None
    swap = len(zs) % 2 == 1
    if swap:
        zs, ys = ys, zs
    rows, cols = len(zs), len(ys)
    if rows % 2 == 1 or cols < 2:
        return None
    walk = [(0, c) for c in range(cols)]
    for r in range(1, rows):
        order = range(cols - 1, 0, -1) if r % 2 == 1 else range(1, cols)
        walk += [(r, c) for c in order]
    walk += [(r, 0) for r in range(rows - 1, 0, -1)]
    cycle = [(zs[r], ys[c]) for r, c in walk]
    if swap:
        cycle = [(y, z) for z, y in cycle]
    return cycle


def ring_order(mesh):
    column = list(mesh.devices[0, :])
    n = len(column)
    try:
        places = [(int(d.coords[2]), int(d.coords[1])) for d in column]
    except Exception:
        return list(range(n))
    cycle = grid_cycle(places)
    if cycle is None or len(set(places)) != n:
        return list(range(n))
    return [places.index(p) for p in cycle]


def lookup(table, index):
    out = jnp.int32(table[0])
    for k in range(1, len(table)):
        out = jnp.where(index == k, jnp.int32(table[k]), out)
    return out


def ring_reduce_scatter(parts, ring, pieces):
    n = len(ring)
    pos_of = [0] * n
    for k, d in enumerate(ring):
        pos_of[d] = k
    me = lax.axis_index("dp")
    pos = lookup(pos_of, me)
    right = [(ring[k], ring[(k + 1) % n]) for k in range(n)]
    left = [(ring[k], ring[(k - 1) % n]) for k in range(n)]
    def block(s, step):
        return lookup(ring, (pos - 1 - s) % n if step < 0 else (pos + 1 + s) % n)

    chains = [(-1 if c % 2 == 0 else 1, c) for c in range(pieces)]
    own = [parts(block(0, step), which, None) for step, which in chains]
    acc = [None] * pieces
    for s in range(n - 1):
        send = [o if x is None else x + o for x, o in zip(acc, own)]
        acc = [
            lax.ppermute(v, "dp", right if step < 0 else left)
            for v, (step, _) in zip(send, chains)
        ]
        own = [
            parts(block(s + 1, step), which, v)
            for v, (step, which) in zip(send, chains)
        ]
    return jnp.concatenate([x + o for x, o in zip(acc, own)], axis=0)


def exchange_four(h_rows, grad_rows):
    a = lax.axis_index("aug")
    rows = h_rows.shape[0]
    sw = h_rows.shape[1] // 4

    def cols(b):
        return lax.dynamic_slice_in_dim(h_rows, b * sw, sw, axis=1)

    over_x = [(i, i ^ 2) for i in range(4)]
    over_core = [(i, i ^ 1) for i in range(4)]
    g_far = lax.ppermute(grad_rows, "aug", over_x)
    g_near = lax.ppermute(grad_rows, "aug", over_core)
    h_far_relay = lax.ppermute(cols(a ^ 3), "aug", over_x)
    h_near = lax.ppermute(cols(a ^ 1), "aug", over_core)
    g_relay = lax.ppermute(g_far, "aug", over_core)
    h_relay = lax.ppermute(h_far_relay, "aug", over_core)
    _, second = lax.optimization_barrier((h_far_relay, cols(a ^ 2)))
    h_far = lax.ppermute(second, "aug", over_x)
    return [
        (a * rows, cols(a), grad_rows),
        ((a ^ 1) * rows, h_near, g_near),
        ((a ^ 2) * rows, h_far, g_far),
        ((a ^ 3) * rows, h_relay, g_relay),
    ]


def butterfly_sum(value, n):
    if n == 4:
        got = {}
        for m in (1, 2, 3):
            got[m] = lax.ppermute(value, "aug", [(i, i ^ m) for i in range(4)])
        return (value + got[1]) + (got[2] + got[3])
    if n & (n - 1):
        return lax.psum(value, "aug")
    bit = 1
    while bit < n:
        value = value + lax.ppermute(value, "aug", [(i, i ^ bit) for i in range(n)])
        bit *= 2
    return value


def per_device(ring, hidden, output_grad, down_weight, first_moment, second_moment, noise):
    views = lax.axis_size("aug")
    groups = lax.axis_size("dp")
    images_here = hidden.shape[1]
    patches = hidden.shape[2]
    width = hidden.shape[3]
    model_width = output_grad.shape[3]
    images_all = images_here * groups
    clip = clip_ratio * math.sqrt(patches * width * model_width / views)
    local_rows = images_here * patches
    h_rows = hidden.reshape(local_rows, width)
    grad_rows = output_grad.reshape(local_rows, model_width)
    if views == 4 and images_here == 1:
        pieces = exchange_four(h_rows, grad_rows)
        slice_width = pieces[0][1].shape[1]
        summed = None
        hidden_grad = jnp.zeros((views * local_rows, slice_width), jnp.bfloat16)
        for at, h_piece, g_piece in pieces:
            term = jnp.dot(h_piece.T, g_piece, preferred_element_type=jnp.float32)
            summed = term if summed is None else summed + term
            back = project_back(g_piece, down_weight).astype(jnp.bfloat16)
            hidden_grad = lax.dynamic_update_slice_in_dim(hidden_grad, back, at, axis=0)
        summed = summed[None]
        hidden_grad = hidden_grad.reshape(views, images_here, patches, slice_width)
    else:
        swapped = lax.all_to_all(h_rows, "aug", split_axis=1, concat_axis=0, tiled=True)
        every = lax.all_gather(grad_rows, "aug", axis=0, tiled=True)
        slice_width = swapped.shape[1]
        h_four = swapped.reshape(views, images_here, patches, slice_width)
        g_four = every.reshape(views, images_here, patches, model_width)
        summed = jnp.einsum("vipf,vipd->ifd", h_four, g_four, preferred_element_type=jnp.float32)
        back_rows = project_back(every, down_weight)
        hidden_grad = back_rows.astype(jnp.bfloat16).reshape(views, images_here, patches, slice_width)
    grads = summed / views
    partial_value = jnp.sum(grads * grads, axis=(1, 2))
    squares = butterfly_sum(partial_value, views)
    image_norms = jnp.sqrt(squares)
    factor = clip / jnp.maximum(image_norms, clip)
    owned_rows = slice_width // groups
    pieces = 4 if owned_rows % 32 == 0 else 2
    half = owned_rows // pieces

    def parts(block, which, after):
        source = grads
        if after is not None:
            _, source = lax.optimization_barrier((after, grads))
        start = block * owned_rows + which * half
        rows = lax.dynamic_slice_in_dim(source, start, half, axis=1)
        return lax.optimization_barrier(jnp.sum(factor[:, None, None] * rows, axis=0))

    owned = ring_reduce_scatter(parts, ring, pieces)
    clipped_mean = owned / images_all
    noisy = clipped_mean + noise_ratio * clip * noise / images_all
    new_first = beta_one * first_moment + (1.0 - beta_one) * noisy
    new_second = beta_two * second_moment + (1.0 - beta_two) * noisy * noisy
    update = (
        new_first
        / (1.0 - beta_one**adam_step)
        / (jnp.sqrt(new_second / (1.0 - beta_two**adam_step)) + adam_eps)
    )
    return (image_norms, clipped_mean, new_first, new_second, update, hidden_grad)


def solution(mesh):
    in_specs = (
        P("aug", "dp", None, None),
        P("aug", "dp", None, None),
        P("aug", None),
        P(("aug", "dp"), None),
        P(("aug", "dp"), None),
        P(("aug", "dp"), None),
    )
    out_specs = (
        P("dp"),
        P(("aug", "dp"), None),
        P(("aug", "dp"), None),
        P(("aug", "dp"), None),
        P(("aug", "dp"), None),
        P(None, "dp", None, "aug"),
    )
    ring = ring_order(mesh)

    def body(*args):
        return per_device(ring, *args)

    return jax.shard_map(
        body, mesh=mesh, in_specs=in_specs, out_specs=out_specs, check_vma=False
    )
```

```python
import math

import jax
import jax.numpy as jnp
from jax import lax
from jax.sharding import PartitionSpec as P

clip_ratio = 1.9
noise_ratio = 0.002
beta_one = 0.9
beta_two = 0.999
adam_step = 10
adam_eps = 1e-08


def project_back(rows, down_weight):
    return lax.dot_general(
        rows, down_weight, (((1,), (1,)), ((), ())), preferred_element_type=jnp.float32
    )


def grid_cycle(points):
    zs = sorted({z for z, _ in points})
    ys = sorted({y for _, y in points})
    if len(zs) * len(ys) != len(points):
        return None
    swap = len(zs) % 2 == 1
    if swap:
        zs, ys = ys, zs
    rows, cols = len(zs), len(ys)
    if rows % 2 == 1 or cols < 2:
        return None
    walk = [(0, c) for c in range(cols)]
    for r in range(1, rows):
        order = range(cols - 1, 0, -1) if r % 2 == 1 else range(1, cols)
        walk += [(r, c) for c in order]
    walk += [(r, 0) for r in range(rows - 1, 0, -1)]
    cycle = [(zs[r], ys[c]) for r, c in walk]
    if swap:
        cycle = [(y, z) for z, y in cycle]
    return cycle


def ring_order(mesh):
    column = list(mesh.devices[0, :])
    n = len(column)
    try:
        places = [(int(d.coords[2]), int(d.coords[1])) for d in column]
    except Exception:
        return list(range(n))
    cycle = grid_cycle(places)
    if cycle is None or len(set(places)) != n:
        return list(range(n))
    return [places.index(p) for p in cycle]


def lookup(table, index):
    out = jnp.int32(table[0])
    for k in range(1, len(table)):
        out = jnp.where(index == k, jnp.int32(table[k]), out)
    return out


def ring_reduce_scatter(parts, ring, pieces, during=None):
    n = len(ring)
    pos_of = [0] * n
    for k, d in enumerate(ring):
        pos_of[d] = k
    me = lax.axis_index("dp")
    pos = lookup(pos_of, me)
    right = [(ring[k], ring[(k + 1) % n]) for k in range(n)]
    left = [(ring[k], ring[(k - 1) % n]) for k in range(n)]
    def block(s, step):
        return lookup(ring, (pos - 1 - s) % n if step < 0 else (pos + 1 + s) % n)

    chains = [(-1 if c % 2 == 0 else 1, c) for c in range(pieces)]
    own = [parts(block(0, step), which, None) for step, which in chains]
    extra = None
    if during is not None:
        extra = during(own)
    acc = [None] * pieces
    for s in range(n - 1):
        send = [o if x is None else x + o for x, o in zip(acc, own)]
        acc = [
            lax.ppermute(v, "dp", right if step < 0 else left)
            for v, (step, _) in zip(send, chains)
        ]
        own = [
            parts(block(s + 1, step), which, v)
            for v, (step, which) in zip(send, chains)
        ]
    return jnp.concatenate([x + o for x, o in zip(acc, own)], axis=0), extra


def exchange_four(h_rows, grad_rows):
    a = lax.axis_index("aug")
    rows = h_rows.shape[0]
    sw = h_rows.shape[1] // 4

    def cols(b):
        return lax.dynamic_slice_in_dim(h_rows, b * sw, sw, axis=1)

    over_x = [(i, i ^ 2) for i in range(4)]
    over_core = [(i, i ^ 1) for i in range(4)]
    g_far = lax.ppermute(grad_rows, "aug", over_x)
    g_near = lax.ppermute(grad_rows, "aug", over_core)
    h_far_relay = lax.ppermute(cols(a ^ 3), "aug", over_x)
    h_near = lax.ppermute(cols(a ^ 1), "aug", over_core)
    g_relay = lax.ppermute(g_far, "aug", over_core)
    h_relay = lax.ppermute(h_far_relay, "aug", over_core)
    _, second = lax.optimization_barrier((h_far_relay, cols(a ^ 2)))
    h_far = lax.ppermute(second, "aug", over_x)
    return [
        (a * rows, cols(a), grad_rows),
        ((a ^ 1) * rows, h_near, g_near),
        ((a ^ 2) * rows, h_far, g_far),
        ((a ^ 3) * rows, h_relay, g_relay),
    ]


def butterfly_sum(value, n):
    if n == 4:
        got = {}
        for m in (1, 2, 3):
            got[m] = lax.ppermute(value, "aug", [(i, i ^ m) for i in range(4)])
        return (value + got[1]) + (got[2] + got[3])
    if n & (n - 1):
        return lax.psum(value, "aug")
    bit = 1
    while bit < n:
        value = value + lax.ppermute(value, "aug", [(i, i ^ bit) for i in range(n)])
        bit *= 2
    return value


def per_device(ring, hidden, output_grad, down_weight, first_moment, second_moment, noise):
    views = lax.axis_size("aug")
    groups = lax.axis_size("dp")
    images_here = hidden.shape[1]
    patches = hidden.shape[2]
    width = hidden.shape[3]
    model_width = output_grad.shape[3]
    images_all = images_here * groups
    clip = clip_ratio * math.sqrt(patches * width * model_width / views)
    local_rows = images_here * patches
    h_rows = hidden.reshape(local_rows, width)
    grad_rows = output_grad.reshape(local_rows, model_width)
    if views == 4 and images_here == 1:
        blocks = exchange_four(h_rows, grad_rows)
        slice_width = blocks[0][1].shape[1]
        summed = None
        for at, h_piece, g_piece in blocks:
            term = jnp.dot(h_piece.T, g_piece, preferred_element_type=jnp.float32)
            summed = term if summed is None else summed + term
        summed = summed[None]

        def project_all(after):
            out = jnp.zeros((views * local_rows, slice_width), jnp.bfloat16)
            for at, _, g_piece in blocks:
                _, g_piece = lax.optimization_barrier((after, g_piece))
                back = project_back(g_piece, down_weight).astype(jnp.bfloat16)
                out = lax.dynamic_update_slice_in_dim(out, back, at, axis=0)
            return out.reshape(views, images_here, patches, slice_width)

        hidden_grad = None
    else:
        swapped = lax.all_to_all(h_rows, "aug", split_axis=1, concat_axis=0, tiled=True)
        every = lax.all_gather(grad_rows, "aug", axis=0, tiled=True)
        slice_width = swapped.shape[1]
        h_four = swapped.reshape(views, images_here, patches, slice_width)
        g_four = every.reshape(views, images_here, patches, model_width)
        summed = jnp.einsum("vipf,vipd->ifd", h_four, g_four, preferred_element_type=jnp.float32)
        back_rows = project_back(every, down_weight)
        hidden_grad = back_rows.astype(jnp.bfloat16).reshape(views, images_here, patches, slice_width)
        project_all = None
    grads = summed / views
    partial_value = jnp.sum(grads * grads, axis=(1, 2))
    squares = butterfly_sum(partial_value, views)
    image_norms = jnp.sqrt(squares)
    factor = clip / jnp.maximum(image_norms, clip)
    owned_rows = slice_width // groups
    pieces = 4 if owned_rows % 32 == 0 else 2
    half = owned_rows // pieces

    def parts(block, which, after):
        source = grads
        if after is not None:
            _, source = lax.optimization_barrier((after, grads))
        start = block * owned_rows + which * half
        rows = lax.dynamic_slice_in_dim(source, start, half, axis=1)
        return lax.optimization_barrier(jnp.sum(factor[:, None, None] * rows, axis=0))

    owned, deferred = ring_reduce_scatter(parts, ring, pieces, project_all)
    if hidden_grad is None:
        hidden_grad = deferred
    clipped_mean = owned / images_all
    noisy = clipped_mean + noise_ratio * clip * noise / images_all
    new_first = beta_one * first_moment + (1.0 - beta_one) * noisy
    new_second = beta_two * second_moment + (1.0 - beta_two) * noisy * noisy
    update = (
        new_first
        / (1.0 - beta_one**adam_step)
        / (jnp.sqrt(new_second / (1.0 - beta_two**adam_step)) + adam_eps)
    )
    return (image_norms, clipped_mean, new_first, new_second, update, hidden_grad)


def solution(mesh):
    in_specs = (
        P("aug", "dp", None, None),
        P("aug", "dp", None, None),
        P("aug", None),
        P(("aug", "dp"), None),
        P(("aug", "dp"), None),
        P(("aug", "dp"), None),
    )
    out_specs = (
        P("dp"),
        P(("aug", "dp"), None),
        P(("aug", "dp"), None),
        P(("aug", "dp"), None),
        P(("aug", "dp"), None),
        P(None, "dp", None, "aug"),
    )
    ring = ring_order(mesh)

    def body(*args):
        return per_device(ring, *args)

    return jax.shard_map(
        body, mesh=mesh, in_specs=in_specs, out_specs=out_specs, check_vma=False
    )
```

```python
import math

import jax
import jax.numpy as jnp
from jax import lax
from jax.sharding import PartitionSpec as P

clip_ratio = 1.9
noise_ratio = 0.002
beta_one = 0.9
beta_two = 0.999
adam_step = 10
adam_eps = 1e-08


def project_back(rows, down_weight):
    return lax.dot_general(
        rows, down_weight, (((1,), (1,)), ((), ())), preferred_element_type=jnp.float32
    )


def grid_cycle(points):
    zs = sorted({z for z, _ in points})
    ys = sorted({y for _, y in points})
    if len(zs) * len(ys) != len(points):
        return None
    swap = len(zs) % 2 == 1
    if swap:
        zs, ys = ys, zs
    rows, cols = len(zs), len(ys)
    if rows % 2 == 1 or cols < 2:
        return None
    walk = [(0, c) for c in range(cols)]
    for r in range(1, rows):
        order = range(cols - 1, 0, -1) if r % 2 == 1 else range(1, cols)
        walk += [(r, c) for c in order]
    walk += [(r, 0) for r in range(rows - 1, 0, -1)]
    cycle = [(zs[r], ys[c]) for r, c in walk]
    if swap:
        cycle = [(y, z) for z, y in cycle]
    return cycle


def ring_order(mesh):
    column = list(mesh.devices[0, :])
    n = len(column)
    try:
        places = [(int(d.coords[2]), int(d.coords[1])) for d in column]
    except Exception:
        return list(range(n))
    cycle = grid_cycle(places)
    if cycle is None or len(set(places)) != n:
        return list(range(n))
    return [places.index(p) for p in cycle]


def lookup(table, index):
    out = jnp.int32(table[0])
    for k in range(1, len(table)):
        out = jnp.where(index == k, jnp.int32(table[k]), out)
    return out


def ring_reduce_scatter(parts, ring, pieces):
    n = len(ring)
    pos_of = [0] * n
    for k, d in enumerate(ring):
        pos_of[d] = k
    me = lax.axis_index("dp")
    pos = lookup(pos_of, me)
    right = [(ring[k], ring[(k + 1) % n]) for k in range(n)]
    left = [(ring[k], ring[(k - 1) % n]) for k in range(n)]
    def block(s, step):
        return lookup(ring, (pos - 1 - s) % n if step < 0 else (pos + 1 + s) % n)

    chains = [(-1 if c % 2 == 0 else 1, c) for c in range(pieces)]
    own = [parts(block(0, step), which, None) for step, which in chains]
    acc = [None] * pieces
    for s in range(n - 1):
        send = [o if x is None else x + o for x, o in zip(acc, own)]
        acc = [
            lax.ppermute(v, "dp", right if step < 0 else left)
            for v, (step, _) in zip(send, chains)
        ]
        own = [
            parts(block(s + 1, step), which, v)
            for v, (step, which) in zip(send, chains)
        ]
    return jnp.concatenate([x + o for x, o in zip(acc, own)], axis=0)


def exchange_four(h_rows, grad_rows):
    a = lax.axis_index("aug")
    rows = h_rows.shape[0]
    sw = h_rows.shape[1] // 4

    def cols(b):
        return lax.dynamic_slice_in_dim(h_rows, b * sw, sw, axis=1)

    over_x = [(i, i ^ 2) for i in range(4)]
    over_core = [(i, i ^ 1) for i in range(4)]
    g_far = lax.ppermute(grad_rows, "aug", over_x)
    h_far_relay = lax.ppermute(cols(a ^ 3), "aug", over_x)
    _, (g_mine, h_mine) = lax.optimization_barrier((h_far_relay, (grad_rows, cols(a ^ 1))))
    g_near = lax.ppermute(g_mine, "aug", over_core)
    h_near = lax.ppermute(h_mine, "aug", over_core)
    g_relay = lax.ppermute(g_far, "aug", over_core)
    h_relay = lax.ppermute(h_far_relay, "aug", over_core)
    _, second = lax.optimization_barrier((h_far_relay, cols(a ^ 2)))
    h_far = lax.ppermute(second, "aug", over_x)
    return [
        (a * rows, cols(a), grad_rows),
        ((a ^ 1) * rows, h_near, g_near),
        ((a ^ 2) * rows, h_far, g_far),
        ((a ^ 3) * rows, h_relay, g_relay),
    ]


def butterfly_sum(value, n):
    if n == 4:
        got = {}
        for m in (1, 2, 3):
            got[m] = lax.ppermute(value, "aug", [(i, i ^ m) for i in range(4)])
        return (value + got[1]) + (got[2] + got[3])
    if n & (n - 1):
        return lax.psum(value, "aug")
    bit = 1
    while bit < n:
        value = value + lax.ppermute(value, "aug", [(i, i ^ bit) for i in range(n)])
        bit *= 2
    return value


def per_device(ring, hidden, output_grad, down_weight, first_moment, second_moment, noise):
    views = lax.axis_size("aug")
    groups = lax.axis_size("dp")
    images_here = hidden.shape[1]
    patches = hidden.shape[2]
    width = hidden.shape[3]
    model_width = output_grad.shape[3]
    images_all = images_here * groups
    clip = clip_ratio * math.sqrt(patches * width * model_width / views)
    local_rows = images_here * patches
    h_rows = hidden.reshape(local_rows, width)
    grad_rows = output_grad.reshape(local_rows, model_width)
    if views == 4 and images_here == 1:
        pieces = exchange_four(h_rows, grad_rows)
        slice_width = pieces[0][1].shape[1]
        summed = None
        hidden_grad = jnp.zeros((views * local_rows, slice_width), jnp.bfloat16)
        for at, h_piece, g_piece in pieces:
            term = jnp.dot(h_piece.T, g_piece, preferred_element_type=jnp.float32)
            summed = term if summed is None else summed + term
            back = project_back(g_piece, down_weight).astype(jnp.bfloat16)
            hidden_grad = lax.dynamic_update_slice_in_dim(hidden_grad, back, at, axis=0)
        summed = summed[None]
        hidden_grad = hidden_grad.reshape(views, images_here, patches, slice_width)
    else:
        swapped = lax.all_to_all(h_rows, "aug", split_axis=1, concat_axis=0, tiled=True)
        every = lax.all_gather(grad_rows, "aug", axis=0, tiled=True)
        slice_width = swapped.shape[1]
        h_four = swapped.reshape(views, images_here, patches, slice_width)
        g_four = every.reshape(views, images_here, patches, model_width)
        summed = jnp.einsum("vipf,vipd->ifd", h_four, g_four, preferred_element_type=jnp.float32)
        back_rows = project_back(every, down_weight)
        hidden_grad = back_rows.astype(jnp.bfloat16).reshape(views, images_here, patches, slice_width)
    grads = summed / views
    partial_value = jnp.sum(grads * grads, axis=(1, 2))
    squares = butterfly_sum(partial_value, views)
    image_norms = jnp.sqrt(squares)
    factor = clip / jnp.maximum(image_norms, clip)
    owned_rows = slice_width // groups
    pieces = 4 if owned_rows % 32 == 0 else 2
    half = owned_rows // pieces

    def parts(block, which, after):
        source = grads
        if after is not None:
            _, source = lax.optimization_barrier((after, grads))
        start = block * owned_rows + which * half
        rows = lax.dynamic_slice_in_dim(source, start, half, axis=1)
        return lax.optimization_barrier(jnp.sum(factor[:, None, None] * rows, axis=0))

    owned = ring_reduce_scatter(parts, ring, pieces)
    clipped_mean = owned / images_all
    noisy = clipped_mean + noise_ratio * clip * noise / images_all
    new_first = beta_one * first_moment + (1.0 - beta_one) * noisy
    new_second = beta_two * second_moment + (1.0 - beta_two) * noisy * noisy
    update = (
        new_first
        / (1.0 - beta_one**adam_step)
        / (jnp.sqrt(new_second / (1.0 - beta_two**adam_step)) + adam_eps)
    )
    return (image_norms, clipped_mean, new_first, new_second, update, hidden_grad)


def solution(mesh):
    in_specs = (
        P("aug", "dp", None, None),
        P("aug", "dp", None, None),
        P("aug", None),
        P(("aug", "dp"), None),
        P(("aug", "dp"), None),
        P(("aug", "dp"), None),
    )
    out_specs = (
        P("dp"),
        P(("aug", "dp"), None),
        P(("aug", "dp"), None),
        P(("aug", "dp"), None),
        P(("aug", "dp"), None),
        P(None, "dp", None, "aug"),
    )
    ring = ring_order(mesh)

    def body(*args):
        return per_device(ring, *args)

    return jax.shard_map(
        body, mesh=mesh, in_specs=in_specs, out_specs=out_specs, check_vma=False
    )
```

```python
import math

import jax
import jax.numpy as jnp
from jax import lax
from jax.sharding import PartitionSpec as P

clip_ratio = 1.9
noise_ratio = 0.002
beta_one = 0.9
beta_two = 0.999
adam_step = 10
adam_eps = 1e-08


def project_back(rows, down_weight):
    return lax.dot_general(
        rows, down_weight, (((1,), (1,)), ((), ())), preferred_element_type=jnp.float32
    )


def grid_cycle(points):
    zs = sorted({z for z, _ in points})
    ys = sorted({y for _, y in points})
    if len(zs) * len(ys) != len(points):
        return None
    swap = len(zs) % 2 == 1
    if swap:
        zs, ys = ys, zs
    rows, cols = len(zs), len(ys)
    if rows % 2 == 1 or cols < 2:
        return None
    walk = [(0, c) for c in range(cols)]
    for r in range(1, rows):
        order = range(cols - 1, 0, -1) if r % 2 == 1 else range(1, cols)
        walk += [(r, c) for c in order]
    walk += [(r, 0) for r in range(rows - 1, 0, -1)]
    cycle = [(zs[r], ys[c]) for r, c in walk]
    if swap:
        cycle = [(y, z) for z, y in cycle]
    return cycle


def ring_order(mesh):
    column = list(mesh.devices[0, :])
    n = len(column)
    try:
        places = [(int(d.coords[2]), int(d.coords[1])) for d in column]
    except Exception:
        return list(range(n))
    cycle = grid_cycle(places)
    if cycle is None or len(set(places)) != n:
        return list(range(n))
    return [places.index(p) for p in cycle]


def lookup(table, index):
    out = jnp.int32(table[0])
    for k in range(1, len(table)):
        out = jnp.where(index == k, jnp.int32(table[k]), out)
    return out


def ring_reduce_scatter(parts, ring, pieces, during=None):
    n = len(ring)
    pos_of = [0] * n
    for k, d in enumerate(ring):
        pos_of[d] = k
    me = lax.axis_index("dp")
    pos = lookup(pos_of, me)
    right = [(ring[k], ring[(k + 1) % n]) for k in range(n)]
    left = [(ring[k], ring[(k - 1) % n]) for k in range(n)]
    def block(s, step):
        return lookup(ring, (pos - 1 - s) % n if step < 0 else (pos + 1 + s) % n)

    chains = [(-1 if c % 2 == 0 else 1, c) for c in range(pieces)]
    own = [parts(block(0, step), which, None) for step, which in chains]
    extra = None
    if during is not None:
        extra = during(own)
    acc = [None] * pieces
    for s in range(n - 1):
        send = [o if x is None else x + o for x, o in zip(acc, own)]
        acc = [
            lax.ppermute(v, "dp", right if step < 0 else left)
            for v, (step, _) in zip(send, chains)
        ]
        own = [
            parts(block(s + 1, step), which, v)
            for v, (step, which) in zip(send, chains)
        ]
    return jnp.concatenate([x + o for x, o in zip(acc, own)], axis=0), extra


def exchange_four(h_rows, grad_rows):
    a = lax.axis_index("aug")
    rows = h_rows.shape[0]
    sw = h_rows.shape[1] // 4

    def cols(b):
        return lax.dynamic_slice_in_dim(h_rows, b * sw, sw, axis=1)

    over_x = [(i, i ^ 2) for i in range(4)]
    over_core = [(i, i ^ 1) for i in range(4)]
    g_far = lax.ppermute(grad_rows, "aug", over_x)
    h_far_relay = lax.ppermute(cols(a ^ 3), "aug", over_x)
    h_far = lax.ppermute(cols(a ^ 2), "aug", over_x)
    _, (g_mine, h_mine, g_fwd, h_fwd) = lax.optimization_barrier(
        ((g_far, h_far_relay, h_far), (grad_rows, cols(a ^ 1), g_far, h_far_relay))
    )
    g_near = lax.ppermute(g_mine, "aug", over_core)
    h_near = lax.ppermute(h_mine, "aug", over_core)
    g_relay = lax.ppermute(g_fwd, "aug", over_core)
    h_relay = lax.ppermute(h_fwd, "aug", over_core)
    return [
        (a * rows, cols(a), grad_rows),
        ((a ^ 1) * rows, h_near, g_near),
        ((a ^ 2) * rows, h_far, g_far),
        ((a ^ 3) * rows, h_relay, g_relay),
    ]


def butterfly_sum(value, n):
    if n == 4:
        got = {}
        for m in (1, 2, 3):
            got[m] = lax.ppermute(value, "aug", [(i, i ^ m) for i in range(4)])
        return (value + got[1]) + (got[2] + got[3])
    if n & (n - 1):
        return lax.psum(value, "aug")
    bit = 1
    while bit < n:
        value = value + lax.ppermute(value, "aug", [(i, i ^ bit) for i in range(n)])
        bit *= 2
    return value


def per_device(ring, hidden, output_grad, down_weight, first_moment, second_moment, noise):
    views = lax.axis_size("aug")
    groups = lax.axis_size("dp")
    images_here = hidden.shape[1]
    patches = hidden.shape[2]
    width = hidden.shape[3]
    model_width = output_grad.shape[3]
    images_all = images_here * groups
    clip = clip_ratio * math.sqrt(patches * width * model_width / views)
    local_rows = images_here * patches
    h_rows = hidden.reshape(local_rows, width)
    grad_rows = output_grad.reshape(local_rows, model_width)
    if views == 4 and images_here == 1:
        blocks = exchange_four(h_rows, grad_rows)
        slice_width = blocks[0][1].shape[1]
        summed = None
        for at, h_piece, g_piece in blocks:
            term = jnp.dot(h_piece.T, g_piece, preferred_element_type=jnp.float32)
            summed = term if summed is None else summed + term
        summed = summed[None]

        def project_all(after):
            out = jnp.zeros((views * local_rows, slice_width), jnp.bfloat16)
            for at, _, g_piece in blocks:
                _, g_piece = lax.optimization_barrier((after, g_piece))
                back = project_back(g_piece, down_weight).astype(jnp.bfloat16)
                out = lax.dynamic_update_slice_in_dim(out, back, at, axis=0)
            return out.reshape(views, images_here, patches, slice_width)

        hidden_grad = None
    else:
        swapped = lax.all_to_all(h_rows, "aug", split_axis=1, concat_axis=0, tiled=True)
        every = lax.all_gather(grad_rows, "aug", axis=0, tiled=True)
        slice_width = swapped.shape[1]
        h_four = swapped.reshape(views, images_here, patches, slice_width)
        g_four = every.reshape(views, images_here, patches, model_width)
        summed = jnp.einsum("vipf,vipd->ifd", h_four, g_four, preferred_element_type=jnp.float32)
        back_rows = project_back(every, down_weight)
        hidden_grad = back_rows.astype(jnp.bfloat16).reshape(views, images_here, patches, slice_width)
        project_all = None
    grads = summed / views
    partial_value = jnp.sum(grads * grads, axis=(1, 2))
    squares = butterfly_sum(partial_value, views)
    image_norms = jnp.sqrt(squares)
    factor = clip / jnp.maximum(image_norms, clip)
    owned_rows = slice_width // groups
    pieces = 4 if owned_rows % 32 == 0 else 2
    half = owned_rows // pieces

    def parts(block, which, after):
        source = grads
        if after is not None:
            _, source = lax.optimization_barrier((after, grads))
        start = block * owned_rows + which * half
        rows = lax.dynamic_slice_in_dim(source, start, half, axis=1)
        return lax.optimization_barrier(jnp.sum(factor[:, None, None] * rows, axis=0))

    owned, deferred = ring_reduce_scatter(parts, ring, pieces, project_all)
    if hidden_grad is None:
        hidden_grad = deferred
    clipped_mean = owned / images_all
    noisy = clipped_mean + noise_ratio * clip * noise / images_all
    new_first = beta_one * first_moment + (1.0 - beta_one) * noisy
    new_second = beta_two * second_moment + (1.0 - beta_two) * noisy * noisy
    update = (
        new_first
        / (1.0 - beta_one**adam_step)
        / (jnp.sqrt(new_second / (1.0 - beta_two**adam_step)) + adam_eps)
    )
    return (image_norms, clipped_mean, new_first, new_second, update, hidden_grad)


def solution(mesh):
    in_specs = (
        P("aug", "dp", None, None),
        P("aug", "dp", None, None),
        P("aug", None),
        P(("aug", "dp"), None),
        P(("aug", "dp"), None),
        P(("aug", "dp"), None),
    )
    out_specs = (
        P("dp"),
        P(("aug", "dp"), None),
        P(("aug", "dp"), None),
        P(("aug", "dp"), None),
        P(("aug", "dp"), None),
        P(None, "dp", None, "aug"),
    )
    ring = ring_order(mesh)

    def body(*args):
        return per_device(ring, *args)

    return jax.shard_map(
        body, mesh=mesh, in_specs=in_specs, out_specs=out_specs, check_vma=False
    )
```

```python
import math

import jax
import jax.numpy as jnp
from jax import lax
from jax.sharding import PartitionSpec as P

clip_ratio = 1.9
noise_ratio = 0.002
beta_one = 0.9
beta_two = 0.999
adam_step = 10
adam_eps = 1e-08


def project_back(rows, down_weight):
    return lax.dot_general(
        rows, down_weight, (((1,), (1,)), ((), ())), preferred_element_type=jnp.float32
    )


def grid_cycle(points):
    zs = sorted({z for z, _ in points})
    ys = sorted({y for _, y in points})
    if len(zs) * len(ys) != len(points):
        return None
    swap = len(zs) % 2 == 1
    if swap:
        zs, ys = ys, zs
    rows, cols = len(zs), len(ys)
    if rows % 2 == 1 or cols < 2:
        return None
    walk = [(0, c) for c in range(cols)]
    for r in range(1, rows):
        order = range(cols - 1, 0, -1) if r % 2 == 1 else range(1, cols)
        walk += [(r, c) for c in order]
    walk += [(r, 0) for r in range(rows - 1, 0, -1)]
    cycle = [(zs[r], ys[c]) for r, c in walk]
    if swap:
        cycle = [(y, z) for z, y in cycle]
    return cycle


def ring_order(mesh):
    column = list(mesh.devices[0, :])
    n = len(column)
    try:
        places = [(int(d.coords[2]), int(d.coords[1])) for d in column]
    except Exception:
        return list(range(n))
    cycle = grid_cycle(places)
    if cycle is None or len(set(places)) != n:
        return list(range(n))
    return [places.index(p) for p in cycle]


def lookup(table, index):
    out = jnp.int32(table[0])
    for k in range(1, len(table)):
        out = jnp.where(index == k, jnp.int32(table[k]), out)
    return out


def ring_reduce_scatter(parts, ring, pieces, during=None):
    n = len(ring)
    pos_of = [0] * n
    for k, d in enumerate(ring):
        pos_of[d] = k
    me = lax.axis_index("dp")
    pos = lookup(pos_of, me)
    right = [(ring[k], ring[(k + 1) % n]) for k in range(n)]
    left = [(ring[k], ring[(k - 1) % n]) for k in range(n)]
    def block(s, step):
        return lookup(ring, (pos - 1 - s) % n if step < 0 else (pos + 1 + s) % n)

    chains = [(-1 if c % 2 == 0 else 1, c) for c in range(pieces)]
    own = [parts(block(0, step), which, None) for step, which in chains]
    extra = None
    if during is not None:
        extra = during(own)
    acc = [None] * pieces
    for s in range(n - 1):
        send = [o if x is None else x + o for x, o in zip(acc, own)]
        acc = [
            lax.ppermute(v, "dp", right if step < 0 else left)
            for v, (step, _) in zip(send, chains)
        ]
        own = [
            parts(block(s + 1, step), which, v)
            for v, (step, which) in zip(send, chains)
        ]
    return jnp.concatenate([x + o for x, o in zip(acc, own)], axis=0), extra


def exchange_four(h_rows, grad_rows):
    a = lax.axis_index("aug")
    rows = h_rows.shape[0]
    sw = h_rows.shape[1] // 4

    def cols(b):
        return lax.dynamic_slice_in_dim(h_rows, b * sw, sw, axis=1)

    over_x = [(i, i ^ 2) for i in range(4)]
    over_core = [(i, i ^ 1) for i in range(4)]
    g_far = lax.ppermute(grad_rows, "aug", over_x)
    h_far_relay = lax.ppermute(cols(a ^ 3), "aug", over_x)
    _, second = lax.optimization_barrier(((g_far, h_far_relay), cols(a ^ 2)))
    h_far = lax.ppermute(second, "aug", over_x)
    g_relay = lax.ppermute(g_far, "aug", over_core)
    h_relay = lax.ppermute(h_far_relay, "aug", over_core)
    _, (g_mine, h_mine) = lax.optimization_barrier((h_far, (grad_rows, cols(a ^ 1))))
    g_near = lax.ppermute(g_mine, "aug", over_core)
    h_near = lax.ppermute(h_mine, "aug", over_core)
    return [
        (a * rows, cols(a), grad_rows),
        ((a ^ 1) * rows, h_near, g_near),
        ((a ^ 2) * rows, h_far, g_far),
        ((a ^ 3) * rows, h_relay, g_relay),
    ]


def butterfly_sum(value, n):
    if n == 4:
        got = {}
        for m in (1, 2, 3):
            got[m] = lax.ppermute(value, "aug", [(i, i ^ m) for i in range(4)])
        return (value + got[1]) + (got[2] + got[3])
    if n & (n - 1):
        return lax.psum(value, "aug")
    bit = 1
    while bit < n:
        value = value + lax.ppermute(value, "aug", [(i, i ^ bit) for i in range(n)])
        bit *= 2
    return value


def per_device(ring, hidden, output_grad, down_weight, first_moment, second_moment, noise):
    views = lax.axis_size("aug")
    groups = lax.axis_size("dp")
    images_here = hidden.shape[1]
    patches = hidden.shape[2]
    width = hidden.shape[3]
    model_width = output_grad.shape[3]
    images_all = images_here * groups
    clip = clip_ratio * math.sqrt(patches * width * model_width / views)
    local_rows = images_here * patches
    h_rows = hidden.reshape(local_rows, width)
    grad_rows = output_grad.reshape(local_rows, model_width)
    if views == 4 and images_here == 1:
        blocks = exchange_four(h_rows, grad_rows)
        slice_width = blocks[0][1].shape[1]
        summed = None
        for at, h_piece, g_piece in blocks:
            term = jnp.dot(h_piece.T, g_piece, preferred_element_type=jnp.float32)
            summed = term if summed is None else summed + term
        summed = summed[None]

        def project_all(after):
            out = jnp.zeros((views * local_rows, slice_width), jnp.bfloat16)
            for at, _, g_piece in blocks:
                _, g_piece = lax.optimization_barrier((after, g_piece))
                back = project_back(g_piece, down_weight).astype(jnp.bfloat16)
                out = lax.dynamic_update_slice_in_dim(out, back, at, axis=0)
            return out.reshape(views, images_here, patches, slice_width)

        hidden_grad = None
    else:
        swapped = lax.all_to_all(h_rows, "aug", split_axis=1, concat_axis=0, tiled=True)
        every = lax.all_gather(grad_rows, "aug", axis=0, tiled=True)
        slice_width = swapped.shape[1]
        h_four = swapped.reshape(views, images_here, patches, slice_width)
        g_four = every.reshape(views, images_here, patches, model_width)
        summed = jnp.einsum("vipf,vipd->ifd", h_four, g_four, preferred_element_type=jnp.float32)
        back_rows = project_back(every, down_weight)
        hidden_grad = back_rows.astype(jnp.bfloat16).reshape(views, images_here, patches, slice_width)
        project_all = None
    grads = summed / views
    partial_value = jnp.sum(grads * grads, axis=(1, 2))
    squares = butterfly_sum(partial_value, views)
    image_norms = jnp.sqrt(squares)
    factor = clip / jnp.maximum(image_norms, clip)
    owned_rows = slice_width // groups
    pieces = 4 if owned_rows % 32 == 0 else 2
    half = owned_rows // pieces

    def parts(block, which, after):
        source = grads
        if after is not None:
            _, source = lax.optimization_barrier((after, grads))
        start = block * owned_rows + which * half
        rows = lax.dynamic_slice_in_dim(source, start, half, axis=1)
        return lax.optimization_barrier(jnp.sum(factor[:, None, None] * rows, axis=0))

    owned, deferred = ring_reduce_scatter(parts, ring, pieces, project_all)
    if hidden_grad is None:
        hidden_grad = deferred
    clipped_mean = owned / images_all
    noisy = clipped_mean + noise_ratio * clip * noise / images_all
    new_first = beta_one * first_moment + (1.0 - beta_one) * noisy
    new_second = beta_two * second_moment + (1.0 - beta_two) * noisy * noisy
    update = (
        new_first
        / (1.0 - beta_one**adam_step)
        / (jnp.sqrt(new_second / (1.0 - beta_two**adam_step)) + adam_eps)
    )
    return (image_norms, clipped_mean, new_first, new_second, update, hidden_grad)


def solution(mesh):
    in_specs = (
        P("aug", "dp", None, None),
        P("aug", "dp", None, None),
        P("aug", None),
        P(("aug", "dp"), None),
        P(("aug", "dp"), None),
        P(("aug", "dp"), None),
    )
    out_specs = (
        P("dp"),
        P(("aug", "dp"), None),
        P(("aug", "dp"), None),
        P(("aug", "dp"), None),
        P(("aug", "dp"), None),
        P(None, "dp", None, "aug"),
    )
    ring = ring_order(mesh)

    def body(*args):
        return per_device(ring, *args)

    return jax.shard_map(
        body, mesh=mesh, in_specs=in_specs, out_specs=out_specs, check_vma=False
    )
```

```python
import math

import jax
import jax.numpy as jnp
from jax import lax
from jax.sharding import PartitionSpec as P

clip_ratio = 1.9
noise_ratio = 0.002
beta_one = 0.9
beta_two = 0.999
adam_step = 10
adam_eps = 1e-08


def project_back(rows, down_weight):
    return lax.dot_general(
        rows, down_weight, (((1,), (1,)), ((), ())), preferred_element_type=jnp.float32
    )


def grid_cycle(points):
    zs = sorted({z for z, _ in points})
    ys = sorted({y for _, y in points})
    if len(zs) * len(ys) != len(points):
        return None
    swap = len(zs) % 2 == 1
    if swap:
        zs, ys = ys, zs
    rows, cols = len(zs), len(ys)
    if rows % 2 == 1 or cols < 2:
        return None
    walk = [(0, c) for c in range(cols)]
    for r in range(1, rows):
        order = range(cols - 1, 0, -1) if r % 2 == 1 else range(1, cols)
        walk += [(r, c) for c in order]
    walk += [(r, 0) for r in range(rows - 1, 0, -1)]
    cycle = [(zs[r], ys[c]) for r, c in walk]
    if swap:
        cycle = [(y, z) for z, y in cycle]
    return cycle


def ring_order(mesh):
    column = list(mesh.devices[0, :])
    n = len(column)
    try:
        places = [(int(d.coords[2]), int(d.coords[1])) for d in column]
    except Exception:
        return list(range(n))
    cycle = grid_cycle(places)
    if cycle is None or len(set(places)) != n:
        return list(range(n))
    return [places.index(p) for p in cycle]


def lookup(table, index):
    out = jnp.int32(table[0])
    for k in range(1, len(table)):
        out = jnp.where(index == k, jnp.int32(table[k]), out)
    return out


def ring_reduce_scatter(parts, ring, pieces, during=None):
    n = len(ring)
    pos_of = [0] * n
    for k, d in enumerate(ring):
        pos_of[d] = k
    me = lax.axis_index("dp")
    pos = lookup(pos_of, me)
    right = [(ring[k], ring[(k + 1) % n]) for k in range(n)]
    left = [(ring[k], ring[(k - 1) % n]) for k in range(n)]
    def block(s, step):
        return lookup(ring, (pos - 1 - s) % n if step < 0 else (pos + 1 + s) % n)

    chains = [(-1 if c % 2 == 0 else 1, c) for c in range(pieces)]
    own = [parts(block(0, step), which, None) for step, which in chains]
    extra = None
    if during is not None:
        extra = during(own)
    acc = [None] * pieces
    for s in range(n - 1):
        send = [o if x is None else x + o for x, o in zip(acc, own)]
        acc = [
            lax.ppermute(v, "dp", right if step < 0 else left)
            for v, (step, _) in zip(send, chains)
        ]
        own = [
            parts(block(s + 1, step), which, v)
            for v, (step, which) in zip(send, chains)
        ]
    return jnp.concatenate([x + o for x, o in zip(acc, own)], axis=0), extra


def exchange_four(h_rows, grad_rows):
    a = lax.axis_index("aug")
    rows = h_rows.shape[0]
    sw = h_rows.shape[1] // 4

    def cols(b):
        return lax.dynamic_slice_in_dim(h_rows, b * sw, sw, axis=1)

    over_x = [(i, i ^ 2) for i in range(4)]
    over_core = [(i, i ^ 1) for i in range(4)]
    g_far = lax.ppermute(grad_rows, "aug", over_x)
    h_far_relay = lax.ppermute(cols(a ^ 3), "aug", over_x)
    _, (g_mine, h_mine) = lax.optimization_barrier((h_far_relay, (grad_rows, cols(a ^ 1))))
    g_near = lax.ppermute(g_mine, "aug", over_core)
    h_near = lax.ppermute(h_mine, "aug", over_core)
    g_relay = lax.ppermute(g_far, "aug", over_core)
    h_relay = lax.ppermute(h_far_relay, "aug", over_core)
    _, second = lax.optimization_barrier((h_far_relay, cols(a ^ 2)))
    h_far = lax.ppermute(second, "aug", over_x)
    return [
        (a * rows, cols(a), grad_rows),
        ((a ^ 1) * rows, h_near, g_near),
        ((a ^ 2) * rows, h_far, g_far),
        ((a ^ 3) * rows, h_relay, g_relay),
    ]


def butterfly_sum(value, n):
    if n == 4:
        got = {}
        for m in (1, 2, 3):
            got[m] = lax.ppermute(value, "aug", [(i, i ^ m) for i in range(4)])
        return (value + got[1]) + (got[2] + got[3])
    if n & (n - 1):
        return lax.psum(value, "aug")
    bit = 1
    while bit < n:
        value = value + lax.ppermute(value, "aug", [(i, i ^ bit) for i in range(n)])
        bit *= 2
    return value


def per_device(ring, hidden, output_grad, down_weight, first_moment, second_moment, noise):
    views = lax.axis_size("aug")
    groups = lax.axis_size("dp")
    images_here = hidden.shape[1]
    patches = hidden.shape[2]
    width = hidden.shape[3]
    model_width = output_grad.shape[3]
    images_all = images_here * groups
    clip = clip_ratio * math.sqrt(patches * width * model_width / views)
    local_rows = images_here * patches
    h_rows = hidden.reshape(local_rows, width)
    grad_rows = output_grad.reshape(local_rows, model_width)
    if views == 4 and images_here == 1:
        blocks = exchange_four(h_rows, grad_rows)
        slice_width = blocks[0][1].shape[1]
        summed = None
        for at, h_piece, g_piece in blocks:
            term = jnp.dot(h_piece.T, g_piece, preferred_element_type=jnp.float32)
            summed = term if summed is None else summed + term
        summed = summed[None]

        def project_all(after):
            out = jnp.zeros((views * local_rows, slice_width), jnp.bfloat16)
            for at, _, g_piece in blocks:
                _, g_piece = lax.optimization_barrier((after, g_piece))
                back = project_back(g_piece, down_weight).astype(jnp.bfloat16)
                out = lax.dynamic_update_slice_in_dim(out, back, at, axis=0)
            return out.reshape(views, images_here, patches, slice_width)

        hidden_grad = None
    else:
        swapped = lax.all_to_all(h_rows, "aug", split_axis=1, concat_axis=0, tiled=True)
        every = lax.all_gather(grad_rows, "aug", axis=0, tiled=True)
        slice_width = swapped.shape[1]
        h_four = swapped.reshape(views, images_here, patches, slice_width)
        g_four = every.reshape(views, images_here, patches, model_width)
        summed = jnp.einsum("vipf,vipd->ifd", h_four, g_four, preferred_element_type=jnp.float32)
        back_rows = project_back(every, down_weight)
        hidden_grad = back_rows.astype(jnp.bfloat16).reshape(views, images_here, patches, slice_width)
        project_all = None
    grads = summed / views
    partial_value = jnp.sum(grads * grads, axis=(1, 2))
    squares = butterfly_sum(partial_value, views)
    image_norms = jnp.sqrt(squares)
    factor = clip / jnp.maximum(image_norms, clip)
    owned_rows = slice_width // groups
    pieces = 4 if owned_rows % 32 == 0 else 2
    half = owned_rows // pieces

    def parts(block, which, after):
        source = grads
        if after is not None:
            _, source = lax.optimization_barrier((after, grads))
        start = block * owned_rows + which * half
        rows = lax.dynamic_slice_in_dim(source, start, half, axis=1)
        return lax.optimization_barrier(jnp.sum(factor[:, None, None] * rows, axis=0))

    owned, deferred = ring_reduce_scatter(parts, ring, pieces, project_all)
    if hidden_grad is None:
        hidden_grad = deferred
    clipped_mean = owned / images_all
    noisy = clipped_mean + noise_ratio * clip * noise / images_all
    new_first = beta_one * first_moment + (1.0 - beta_one) * noisy
    new_second = beta_two * second_moment + (1.0 - beta_two) * noisy * noisy
    update = (
        new_first
        / (1.0 - beta_one**adam_step)
        / (jnp.sqrt(new_second / (1.0 - beta_two**adam_step)) + adam_eps)
    )
    return (image_norms, clipped_mean, new_first, new_second, update, hidden_grad)


def solution(mesh):
    in_specs = (
        P("aug", "dp", None, None),
        P("aug", "dp", None, None),
        P("aug", None),
        P(("aug", "dp"), None),
        P(("aug", "dp"), None),
        P(("aug", "dp"), None),
    )
    out_specs = (
        P("dp"),
        P(("aug", "dp"), None),
        P(("aug", "dp"), None),
        P(("aug", "dp"), None),
        P(("aug", "dp"), None),
        P(None, "dp", None, "aug"),
    )
    ring = ring_order(mesh)

    def body(*args):
        return per_device(ring, *args)

    return jax.shard_map(
        body, mesh=mesh, in_specs=in_specs, out_specs=out_specs, check_vma=False
    )
```

```python
import math

import jax
import jax.numpy as jnp
from jax import lax
from jax.sharding import PartitionSpec as P

clip_ratio = 1.9
noise_ratio = 0.002
beta_one = 0.9
beta_two = 0.999
adam_step = 10
adam_eps = 1e-08


def project_back(rows, down_weight):
    return lax.dot_general(
        rows, down_weight, (((1,), (1,)), ((), ())), preferred_element_type=jnp.float32
    )


def grid_cycle(points):
    zs = sorted({z for z, _ in points})
    ys = sorted({y for _, y in points})
    if len(zs) * len(ys) != len(points):
        return None
    swap = len(zs) % 2 == 1
    if swap:
        zs, ys = ys, zs
    rows, cols = len(zs), len(ys)
    if rows % 2 == 1 or cols < 2:
        return None
    walk = [(0, c) for c in range(cols)]
    for r in range(1, rows):
        order = range(cols - 1, 0, -1) if r % 2 == 1 else range(1, cols)
        walk += [(r, c) for c in order]
    walk += [(r, 0) for r in range(rows - 1, 0, -1)]
    cycle = [(zs[r], ys[c]) for r, c in walk]
    if swap:
        cycle = [(y, z) for z, y in cycle]
    return cycle


def ring_order(mesh):
    column = list(mesh.devices[0, :])
    n = len(column)
    try:
        places = [(int(d.coords[2]), int(d.coords[1])) for d in column]
    except Exception:
        return list(range(n))
    cycle = grid_cycle(places)
    if cycle is None or len(set(places)) != n:
        return list(range(n))
    return [places.index(p) for p in cycle]


def lookup(table, index):
    out = jnp.int32(table[0])
    for k in range(1, len(table)):
        out = jnp.where(index == k, jnp.int32(table[k]), out)
    return out


def ring_reduce_scatter(parts, ring, pieces, during=None):
    n = len(ring)
    pos_of = [0] * n
    for k, d in enumerate(ring):
        pos_of[d] = k
    me = lax.axis_index("dp")
    pos = lookup(pos_of, me)
    right = [(ring[k], ring[(k + 1) % n]) for k in range(n)]
    left = [(ring[k], ring[(k - 1) % n]) for k in range(n)]
    def block(s, step):
        return lookup(ring, (pos - 1 - s) % n if step < 0 else (pos + 1 + s) % n)

    chains = [(-1 if c % 2 == 0 else 1, c) for c in range(pieces)]
    own = [parts(block(0, step), which, None) for step, which in chains]
    extra = []
    acc = [None] * pieces
    for s in range(n - 1):
        send = [o if x is None else x + o for x, o in zip(acc, own)]
        if during is not None:
            extra.append(during(s, send))
        acc = [
            lax.ppermute(v, "dp", right if step < 0 else left)
            for v, (step, _) in zip(send, chains)
        ]
        own = [
            parts(block(s + 1, step), which, v)
            for v, (step, which) in zip(send, chains)
        ]
    return jnp.concatenate([x + o for x, o in zip(acc, own)], axis=0), extra


def exchange_four(h_rows, grad_rows):
    a = lax.axis_index("aug")
    rows = h_rows.shape[0]
    sw = h_rows.shape[1] // 4

    def cols(b):
        return lax.dynamic_slice_in_dim(h_rows, b * sw, sw, axis=1)

    over_x = [(i, i ^ 2) for i in range(4)]
    over_core = [(i, i ^ 1) for i in range(4)]
    g_far = lax.ppermute(grad_rows, "aug", over_x)
    h_far_relay = lax.ppermute(cols(a ^ 3), "aug", over_x)
    _, (g_mine, h_mine) = lax.optimization_barrier((h_far_relay, (grad_rows, cols(a ^ 1))))
    g_near = lax.ppermute(g_mine, "aug", over_core)
    h_near = lax.ppermute(h_mine, "aug", over_core)
    g_relay = lax.ppermute(g_far, "aug", over_core)
    h_relay = lax.ppermute(h_far_relay, "aug", over_core)
    _, second = lax.optimization_barrier((h_far_relay, cols(a ^ 2)))
    h_far = lax.ppermute(second, "aug", over_x)
    return [
        (a * rows, cols(a), grad_rows),
        ((a ^ 1) * rows, h_near, g_near),
        ((a ^ 2) * rows, h_far, g_far),
        ((a ^ 3) * rows, h_relay, g_relay),
    ]


def butterfly_sum(value, n):
    if n == 4:
        got = {}
        for m in (1, 2, 3):
            got[m] = lax.ppermute(value, "aug", [(i, i ^ m) for i in range(4)])
        return (value + got[1]) + (got[2] + got[3])
    if n & (n - 1):
        return lax.psum(value, "aug")
    bit = 1
    while bit < n:
        value = value + lax.ppermute(value, "aug", [(i, i ^ bit) for i in range(n)])
        bit *= 2
    return value


def per_device(ring, hidden, output_grad, down_weight, first_moment, second_moment, noise):
    views = lax.axis_size("aug")
    groups = lax.axis_size("dp")
    images_here = hidden.shape[1]
    patches = hidden.shape[2]
    width = hidden.shape[3]
    model_width = output_grad.shape[3]
    images_all = images_here * groups
    clip = clip_ratio * math.sqrt(patches * width * model_width / views)
    local_rows = images_here * patches
    h_rows = hidden.reshape(local_rows, width)
    grad_rows = output_grad.reshape(local_rows, model_width)
    if views == 4 and images_here == 1:
        blocks = exchange_four(h_rows, grad_rows)
        slice_width = blocks[0][1].shape[1]
        summed = None
        for at, h_piece, g_piece in blocks:
            term = jnp.dot(h_piece.T, g_piece, preferred_element_type=jnp.float32)
            summed = term if summed is None else summed + term
        summed = summed[None]

        def project_all(step, after):
            if step >= len(blocks):
                return None
            at, _, g_piece = blocks[step]
            _, g_piece = lax.optimization_barrier((after, g_piece))
            return at, project_back(g_piece, down_weight).astype(jnp.bfloat16)

        hidden_grad = None
    else:
        swapped = lax.all_to_all(h_rows, "aug", split_axis=1, concat_axis=0, tiled=True)
        every = lax.all_gather(grad_rows, "aug", axis=0, tiled=True)
        slice_width = swapped.shape[1]
        h_four = swapped.reshape(views, images_here, patches, slice_width)
        g_four = every.reshape(views, images_here, patches, model_width)
        summed = jnp.einsum("vipf,vipd->ifd", h_four, g_four, preferred_element_type=jnp.float32)
        back_rows = project_back(every, down_weight)
        hidden_grad = back_rows.astype(jnp.bfloat16).reshape(views, images_here, patches, slice_width)
        project_all = None
    grads = summed / views
    partial_value = jnp.sum(grads * grads, axis=(1, 2))
    squares = butterfly_sum(partial_value, views)
    image_norms = jnp.sqrt(squares)
    factor = clip / jnp.maximum(image_norms, clip)
    owned_rows = slice_width // groups
    pieces = 4 if owned_rows % 32 == 0 else 2
    half = owned_rows // pieces

    def parts(block, which, after):
        source = grads
        if after is not None:
            _, source = lax.optimization_barrier((after, grads))
        start = block * owned_rows + which * half
        rows = lax.dynamic_slice_in_dim(source, start, half, axis=1)
        return lax.optimization_barrier(jnp.sum(factor[:, None, None] * rows, axis=0))

    owned, deferred = ring_reduce_scatter(parts, ring, pieces, project_all)
    if hidden_grad is None:
        out = jnp.zeros((views * local_rows, slice_width), jnp.bfloat16)
        for item in deferred:
            if item is not None:
                out = lax.dynamic_update_slice_in_dim(out, item[1], item[0], axis=0)
        hidden_grad = out.reshape(views, images_here, patches, slice_width)
    clipped_mean = owned / images_all
    noisy = clipped_mean + noise_ratio * clip * noise / images_all
    new_first = beta_one * first_moment + (1.0 - beta_one) * noisy
    new_second = beta_two * second_moment + (1.0 - beta_two) * noisy * noisy
    update = (
        new_first
        / (1.0 - beta_one**adam_step)
        / (jnp.sqrt(new_second / (1.0 - beta_two**adam_step)) + adam_eps)
    )
    return (image_norms, clipped_mean, new_first, new_second, update, hidden_grad)


def solution(mesh):
    in_specs = (
        P("aug", "dp", None, None),
        P("aug", "dp", None, None),
        P("aug", None),
        P(("aug", "dp"), None),
        P(("aug", "dp"), None),
        P(("aug", "dp"), None),
    )
    out_specs = (
        P("dp"),
        P(("aug", "dp"), None),
        P(("aug", "dp"), None),
        P(("aug", "dp"), None),
        P(("aug", "dp"), None),
        P(None, "dp", None, "aug"),
    )
    ring = ring_order(mesh)

    def body(*args):
        return per_device(ring, *args)

    return jax.shard_map(
        body, mesh=mesh, in_specs=in_specs, out_specs=out_specs, check_vma=False
    )
```

```python
import math

import jax
import jax.numpy as jnp
from jax import lax
from jax.sharding import PartitionSpec as P

clip_ratio = 1.9
noise_ratio = 0.002
beta_one = 0.9
beta_two = 0.999
adam_step = 10
adam_eps = 1e-08


def project_back(rows, down_weight):
    return lax.dot_general(
        rows, down_weight, (((1,), (1,)), ((), ())), preferred_element_type=jnp.float32
    )


def grid_cycle(points):
    zs = sorted({z for z, _ in points})
    ys = sorted({y for _, y in points})
    if len(zs) * len(ys) != len(points):
        return None
    swap = len(zs) % 2 == 1
    if swap:
        zs, ys = ys, zs
    rows, cols = len(zs), len(ys)
    if rows % 2 == 1 or cols < 2:
        return None
    walk = [(0, c) for c in range(cols)]
    for r in range(1, rows):
        order = range(cols - 1, 0, -1) if r % 2 == 1 else range(1, cols)
        walk += [(r, c) for c in order]
    walk += [(r, 0) for r in range(rows - 1, 0, -1)]
    cycle = [(zs[r], ys[c]) for r, c in walk]
    if swap:
        cycle = [(y, z) for z, y in cycle]
    return cycle


def ring_order(mesh):
    column = list(mesh.devices[0, :])
    n = len(column)
    try:
        places = [(int(d.coords[2]), int(d.coords[1])) for d in column]
    except Exception:
        return list(range(n))
    cycle = grid_cycle(places)
    if cycle is None or len(set(places)) != n:
        return list(range(n))
    return [places.index(p) for p in cycle]


def lookup(table, index):
    out = jnp.int32(table[0])
    for k in range(1, len(table)):
        out = jnp.where(index == k, jnp.int32(table[k]), out)
    return out


def ring_reduce_scatter(parts, ring, pieces, during=None):
    n = len(ring)
    pos_of = [0] * n
    for k, d in enumerate(ring):
        pos_of[d] = k
    me = lax.axis_index("dp")
    pos = lookup(pos_of, me)
    right = [(ring[k], ring[(k + 1) % n]) for k in range(n)]
    left = [(ring[k], ring[(k - 1) % n]) for k in range(n)]
    def block(s, step):
        return lookup(ring, (pos - 1 - s) % n if step < 0 else (pos + 1 + s) % n)

    chains = [(-1 if c % 2 == 0 else 1, c) for c in range(pieces)]
    own = [parts(block(0, step), which, None) for step, which in chains]
    extra = []
    acc = [None] * pieces
    for s in range(n - 1):
        send = [o if x is None else x + o for x, o in zip(acc, own)]
        if during is not None:
            extra.append(during(s, send))
        acc = [
            lax.ppermute(v, "dp", right if step < 0 else left)
            for v, (step, _) in zip(send, chains)
        ]
        own = [
            parts(block(s + 1, step), which, v)
            for v, (step, which) in zip(send, chains)
        ]
    return jnp.concatenate([x + o for x, o in zip(acc, own)], axis=0), extra


def exchange_four(h_rows, grad_rows):
    a = lax.axis_index("aug")
    rows = h_rows.shape[0]
    sw = h_rows.shape[1] // 4

    def cols(b):
        return lax.dynamic_slice_in_dim(h_rows, b * sw, sw, axis=1)

    over_x = [(i, i ^ 2) for i in range(4)]
    over_core = [(i, i ^ 1) for i in range(4)]
    g_far = lax.ppermute(grad_rows, "aug", over_x)
    other = lax.dynamic_slice_in_dim(h_rows, ((a ^ 2) & ~1) * sw, 2 * sw, axis=1)
    h_pair = lax.ppermute(other, "aug", over_x)
    h_far = lax.dynamic_slice_in_dim(h_pair, (a & 1) * sw, sw, axis=1)
    h_fwd = lax.dynamic_slice_in_dim(h_pair, ((a & 1) ^ 1) * sw, sw, axis=1)
    _, (g_mine, h_mine) = lax.optimization_barrier((h_pair, (grad_rows, cols(a ^ 1))))
    g_near = lax.ppermute(g_mine, "aug", over_core)
    h_near = lax.ppermute(h_mine, "aug", over_core)
    g_relay = lax.ppermute(g_far, "aug", over_core)
    h_relay = lax.ppermute(h_fwd, "aug", over_core)
    return [
        (a * rows, cols(a), grad_rows),
        ((a ^ 1) * rows, h_near, g_near),
        ((a ^ 2) * rows, h_far, g_far),
        ((a ^ 3) * rows, h_relay, g_relay),
    ]


def butterfly_sum(value, n):
    if n == 4:
        got = {}
        for m in (1, 2, 3):
            got[m] = lax.ppermute(value, "aug", [(i, i ^ m) for i in range(4)])
        return (value + got[1]) + (got[2] + got[3])
    if n & (n - 1):
        return lax.psum(value, "aug")
    bit = 1
    while bit < n:
        value = value + lax.ppermute(value, "aug", [(i, i ^ bit) for i in range(n)])
        bit *= 2
    return value


def per_device(ring, hidden, output_grad, down_weight, first_moment, second_moment, noise):
    views = lax.axis_size("aug")
    groups = lax.axis_size("dp")
    images_here = hidden.shape[1]
    patches = hidden.shape[2]
    width = hidden.shape[3]
    model_width = output_grad.shape[3]
    images_all = images_here * groups
    clip = clip_ratio * math.sqrt(patches * width * model_width / views)
    local_rows = images_here * patches
    h_rows = hidden.reshape(local_rows, width)
    grad_rows = output_grad.reshape(local_rows, model_width)
    if views == 4 and images_here == 1:
        blocks = exchange_four(h_rows, grad_rows)
        slice_width = blocks[0][1].shape[1]
        summed = None
        for at, h_piece, g_piece in blocks:
            term = jnp.dot(h_piece.T, g_piece, preferred_element_type=jnp.float32)
            summed = term if summed is None else summed + term
        summed = summed[None]

        def project_all(step, after):
            if step >= len(blocks):
                return None
            at, _, g_piece = blocks[step]
            _, g_piece = lax.optimization_barrier((after, g_piece))
            return at, project_back(g_piece, down_weight).astype(jnp.bfloat16)

        hidden_grad = None
    else:
        swapped = lax.all_to_all(h_rows, "aug", split_axis=1, concat_axis=0, tiled=True)
        every = lax.all_gather(grad_rows, "aug", axis=0, tiled=True)
        slice_width = swapped.shape[1]
        h_four = swapped.reshape(views, images_here, patches, slice_width)
        g_four = every.reshape(views, images_here, patches, model_width)
        summed = jnp.einsum("vipf,vipd->ifd", h_four, g_four, preferred_element_type=jnp.float32)
        back_rows = project_back(every, down_weight)
        hidden_grad = back_rows.astype(jnp.bfloat16).reshape(views, images_here, patches, slice_width)
        project_all = None
    grads = summed / views
    partial_value = jnp.sum(grads * grads, axis=(1, 2))
    squares = butterfly_sum(partial_value, views)
    image_norms = jnp.sqrt(squares)
    factor = clip / jnp.maximum(image_norms, clip)
    owned_rows = slice_width // groups
    pieces = 4 if owned_rows % 32 == 0 else 2
    half = owned_rows // pieces

    def parts(block, which, after):
        source = grads
        if after is not None:
            _, source = lax.optimization_barrier((after, grads))
        start = block * owned_rows + which * half
        rows = lax.dynamic_slice_in_dim(source, start, half, axis=1)
        return lax.optimization_barrier(jnp.sum(factor[:, None, None] * rows, axis=0))

    owned, deferred = ring_reduce_scatter(parts, ring, pieces, project_all)
    if hidden_grad is None:
        out = jnp.zeros((views * local_rows, slice_width), jnp.bfloat16)
        for item in deferred:
            if item is not None:
                out = lax.dynamic_update_slice_in_dim(out, item[1], item[0], axis=0)
        hidden_grad = out.reshape(views, images_here, patches, slice_width)
    clipped_mean = owned / images_all
    noisy = clipped_mean + noise_ratio * clip * noise / images_all
    new_first = beta_one * first_moment + (1.0 - beta_one) * noisy
    new_second = beta_two * second_moment + (1.0 - beta_two) * noisy * noisy
    update = (
        new_first
        / (1.0 - beta_one**adam_step)
        / (jnp.sqrt(new_second / (1.0 - beta_two**adam_step)) + adam_eps)
    )
    return (image_norms, clipped_mean, new_first, new_second, update, hidden_grad)


def solution(mesh):
    in_specs = (
        P("aug", "dp", None, None),
        P("aug", "dp", None, None),
        P("aug", None),
        P(("aug", "dp"), None),
        P(("aug", "dp"), None),
        P(("aug", "dp"), None),
    )
    out_specs = (
        P("dp"),
        P(("aug", "dp"), None),
        P(("aug", "dp"), None),
        P(("aug", "dp"), None),
        P(("aug", "dp"), None),
        P(None, "dp", None, "aug"),
    )
    ring = ring_order(mesh)

    def body(*args):
        return per_device(ring, *args)

    return jax.shard_map(
        body, mesh=mesh, in_specs=in_specs, out_specs=out_specs, check_vma=False
    )
```

```python
import math

import jax
import jax.numpy as jnp
from jax import lax
from jax.sharding import PartitionSpec as P

clip_ratio = 1.9
noise_ratio = 0.002
beta_one = 0.9
beta_two = 0.999
adam_step = 10
adam_eps = 1e-08


def project_back(rows, down_weight):
    return lax.dot_general(
        rows, down_weight, (((1,), (1,)), ((), ())), preferred_element_type=jnp.float32
    )


def grid_cycle(points):
    zs = sorted({z for z, _ in points})
    ys = sorted({y for _, y in points})
    if len(zs) * len(ys) != len(points):
        return None
    swap = len(zs) % 2 == 1
    if swap:
        zs, ys = ys, zs
    rows, cols = len(zs), len(ys)
    if rows % 2 == 1 or cols < 2:
        return None
    walk = [(0, c) for c in range(cols)]
    for r in range(1, rows):
        order = range(cols - 1, 0, -1) if r % 2 == 1 else range(1, cols)
        walk += [(r, c) for c in order]
    walk += [(r, 0) for r in range(rows - 1, 0, -1)]
    cycle = [(zs[r], ys[c]) for r, c in walk]
    if swap:
        cycle = [(y, z) for z, y in cycle]
    return cycle


def ring_order(mesh):
    column = list(mesh.devices[0, :])
    n = len(column)
    try:
        places = [(int(d.coords[2]), int(d.coords[1])) for d in column]
    except Exception:
        return list(range(n))
    cycle = grid_cycle(places)
    if cycle is None or len(set(places)) != n:
        return list(range(n))
    return [places.index(p) for p in cycle]


def lookup(table, index):
    out = jnp.int32(table[0])
    for k in range(1, len(table)):
        out = jnp.where(index == k, jnp.int32(table[k]), out)
    return out


def ring_reduce_scatter(parts, ring, pieces, during=None):
    n = len(ring)
    pos_of = [0] * n
    for k, d in enumerate(ring):
        pos_of[d] = k
    me = lax.axis_index("dp")
    pos = lookup(pos_of, me)
    right = [(ring[k], ring[(k + 1) % n]) for k in range(n)]
    left = [(ring[k], ring[(k - 1) % n]) for k in range(n)]
    def block(s, step):
        return lookup(ring, (pos - 1 - s) % n if step < 0 else (pos + 1 + s) % n)

    chains = [(-1 if c % 2 == 0 else 1, c) for c in range(pieces)]
    own = [parts(block(0, step), which, None) for step, which in chains]
    extra = []
    acc = [None] * pieces
    for s in range(n - 1):
        send = [o if x is None else x + o for x, o in zip(acc, own)]
        if during is not None:
            extra.append(during(s, send))
        acc = [
            lax.ppermute(v, "dp", right if step < 0 else left)
            for v, (step, _) in zip(send, chains)
        ]
        own = [
            parts(block(s + 1, step), which, v)
            for v, (step, which) in zip(send, chains)
        ]
    return jnp.concatenate([x + o for x, o in zip(acc, own)], axis=0), extra


def exchange_four(h_rows, grad_rows):
    a = lax.axis_index("aug")
    rows = h_rows.shape[0]
    sw = h_rows.shape[1] // 4

    def cols(b):
        return lax.dynamic_slice_in_dim(h_rows, b * sw, sw, axis=1)

    over_x = [(i, i ^ 2) for i in range(4)]
    over_core = [(i, i ^ 1) for i in range(4)]
    g_far = lax.ppermute(grad_rows, "aug", over_x)
    h_far_relay = lax.ppermute(cols(a ^ 3), "aug", over_x)
    g_relay = lax.ppermute(g_far, "aug", over_core)
    h_relay = lax.ppermute(h_far_relay, "aug", over_core)
    _, second = lax.optimization_barrier((h_far_relay, cols(a ^ 2)))
    h_far = lax.ppermute(second, "aug", over_x)
    _, (g_mine, h_mine) = lax.optimization_barrier((h_far, (grad_rows, cols(a ^ 1))))
    g_near = lax.ppermute(g_mine, "aug", over_core)
    h_near = lax.ppermute(h_mine, "aug", over_core)
    return [
        (a * rows, cols(a), grad_rows),
        ((a ^ 1) * rows, h_near, g_near),
        ((a ^ 2) * rows, h_far, g_far),
        ((a ^ 3) * rows, h_relay, g_relay),
    ]


def butterfly_sum(value, n):
    if n == 4:
        got = {}
        for m in (1, 2, 3):
            got[m] = lax.ppermute(value, "aug", [(i, i ^ m) for i in range(4)])
        return (value + got[1]) + (got[2] + got[3])
    if n & (n - 1):
        return lax.psum(value, "aug")
    bit = 1
    while bit < n:
        value = value + lax.ppermute(value, "aug", [(i, i ^ bit) for i in range(n)])
        bit *= 2
    return value


def per_device(ring, hidden, output_grad, down_weight, first_moment, second_moment, noise):
    views = lax.axis_size("aug")
    groups = lax.axis_size("dp")
    images_here = hidden.shape[1]
    patches = hidden.shape[2]
    width = hidden.shape[3]
    model_width = output_grad.shape[3]
    images_all = images_here * groups
    clip = clip_ratio * math.sqrt(patches * width * model_width / views)
    local_rows = images_here * patches
    h_rows = hidden.reshape(local_rows, width)
    grad_rows = output_grad.reshape(local_rows, model_width)
    if views == 4 and images_here == 1:
        blocks = exchange_four(h_rows, grad_rows)
        slice_width = blocks[0][1].shape[1]
        summed = None
        for at, h_piece, g_piece in blocks:
            term = jnp.dot(h_piece.T, g_piece, preferred_element_type=jnp.float32)
            summed = term if summed is None else summed + term
        summed = summed[None]

        def project_all(step, after):
            if step >= len(blocks):
                return None
            at, _, g_piece = blocks[step]
            _, g_piece = lax.optimization_barrier((after, g_piece))
            return at, project_back(g_piece, down_weight).astype(jnp.bfloat16)

        hidden_grad = None
    else:
        swapped = lax.all_to_all(h_rows, "aug", split_axis=1, concat_axis=0, tiled=True)
        every = lax.all_gather(grad_rows, "aug", axis=0, tiled=True)
        slice_width = swapped.shape[1]
        h_four = swapped.reshape(views, images_here, patches, slice_width)
        g_four = every.reshape(views, images_here, patches, model_width)
        summed = jnp.einsum("vipf,vipd->ifd", h_four, g_four, preferred_element_type=jnp.float32)
        back_rows = project_back(every, down_weight)
        hidden_grad = back_rows.astype(jnp.bfloat16).reshape(views, images_here, patches, slice_width)
        project_all = None
    grads = summed / views
    partial_value = jnp.sum(grads * grads, axis=(1, 2))
    squares = butterfly_sum(partial_value, views)
    image_norms = jnp.sqrt(squares)
    factor = clip / jnp.maximum(image_norms, clip)
    owned_rows = slice_width // groups
    pieces = 4 if owned_rows % 32 == 0 else 2
    half = owned_rows // pieces

    def parts(block, which, after):
        source = grads
        if after is not None:
            _, source = lax.optimization_barrier((after, grads))
        start = block * owned_rows + which * half
        rows = lax.dynamic_slice_in_dim(source, start, half, axis=1)
        return lax.optimization_barrier(jnp.sum(factor[:, None, None] * rows, axis=0))

    owned, deferred = ring_reduce_scatter(parts, ring, pieces, project_all)
    if hidden_grad is None:
        out = jnp.zeros((views * local_rows, slice_width), jnp.bfloat16)
        for item in deferred:
            if item is not None:
                out = lax.dynamic_update_slice_in_dim(out, item[1], item[0], axis=0)
        hidden_grad = out.reshape(views, images_here, patches, slice_width)
    clipped_mean = owned / images_all
    noisy = clipped_mean + noise_ratio * clip * noise / images_all
    new_first = beta_one * first_moment + (1.0 - beta_one) * noisy
    new_second = beta_two * second_moment + (1.0 - beta_two) * noisy * noisy
    update = (
        new_first
        / (1.0 - beta_one**adam_step)
        / (jnp.sqrt(new_second / (1.0 - beta_two**adam_step)) + adam_eps)
    )
    return (image_norms, clipped_mean, new_first, new_second, update, hidden_grad)


def solution(mesh):
    in_specs = (
        P("aug", "dp", None, None),
        P("aug", "dp", None, None),
        P("aug", None),
        P(("aug", "dp"), None),
        P(("aug", "dp"), None),
        P(("aug", "dp"), None),
    )
    out_specs = (
        P("dp"),
        P(("aug", "dp"), None),
        P(("aug", "dp"), None),
        P(("aug", "dp"), None),
        P(("aug", "dp"), None),
        P(None, "dp", None, "aug"),
    )
    ring = ring_order(mesh)

    def body(*args):
        return per_device(ring, *args)

    return jax.shard_map(
        body, mesh=mesh, in_specs=in_specs, out_specs=out_specs, check_vma=False
    )
```

```python
import math

import jax
import jax.numpy as jnp
from jax import lax
from jax.sharding import PartitionSpec as P

clip_ratio = 1.9
noise_ratio = 0.002
beta_one = 0.9
beta_two = 0.999
adam_step = 10
adam_eps = 1e-08


def project_back(rows, down_weight):
    return lax.dot_general(
        rows, down_weight, (((1,), (1,)), ((), ())), preferred_element_type=jnp.float32
    )


def grid_cycle(points):
    zs = sorted({z for z, _ in points})
    ys = sorted({y for _, y in points})
    if len(zs) * len(ys) != len(points):
        return None
    swap = len(zs) % 2 == 1
    if swap:
        zs, ys = ys, zs
    rows, cols = len(zs), len(ys)
    if rows % 2 == 1 or cols < 2:
        return None
    walk = [(0, c) for c in range(cols)]
    for r in range(1, rows):
        order = range(cols - 1, 0, -1) if r % 2 == 1 else range(1, cols)
        walk += [(r, c) for c in order]
    walk += [(r, 0) for r in range(rows - 1, 0, -1)]
    cycle = [(zs[r], ys[c]) for r, c in walk]
    if swap:
        cycle = [(y, z) for z, y in cycle]
    return cycle


def ring_order(mesh):
    column = list(mesh.devices[0, :])
    n = len(column)
    try:
        places = [(int(d.coords[2]), int(d.coords[1])) for d in column]
    except Exception:
        return list(range(n))
    cycle = grid_cycle(places)
    if cycle is None or len(set(places)) != n:
        return list(range(n))
    return [places.index(p) for p in cycle]


def lookup(table, index):
    out = jnp.int32(table[0])
    for k in range(1, len(table)):
        out = jnp.where(index == k, jnp.int32(table[k]), out)
    return out


def ring_reduce_scatter(parts, ring, pieces, during=None):
    n = len(ring)
    pos_of = [0] * n
    for k, d in enumerate(ring):
        pos_of[d] = k
    me = lax.axis_index("dp")
    pos = lookup(pos_of, me)
    right = [(ring[k], ring[(k + 1) % n]) for k in range(n)]
    left = [(ring[k], ring[(k - 1) % n]) for k in range(n)]
    def block(s, step):
        return lookup(ring, (pos - 1 - s) % n if step < 0 else (pos + 1 + s) % n)

    chains = [(-1 if c % 2 == 0 else 1, c) for c in range(pieces)]
    own = [parts(block(0, step), which, None) for step, which in chains]
    extra = []
    acc = [None] * pieces
    for s in range(n - 1):
        send = [o if x is None else x + o for x, o in zip(acc, own)]
        if during is not None:
            extra.append(during(s, send))
        acc = [
            lax.ppermute(v, "dp", right if step < 0 else left)
            for v, (step, _) in zip(send, chains)
        ]
        own = [
            parts(block(s + 1, step), which, v)
            for v, (step, which) in zip(send, chains)
        ]
    return jnp.concatenate([x + o for x, o in zip(acc, own)], axis=0), extra


def exchange_four(h_rows, grad_rows):
    a = lax.axis_index("aug")
    rows = h_rows.shape[0]
    sw = h_rows.shape[1] // 4

    def cols(b):
        return lax.dynamic_slice_in_dim(h_rows, b * sw, sw, axis=1)

    over_x = [(i, i ^ 2) for i in range(4)]
    over_core = [(i, i ^ 1) for i in range(4)]
    g_far = lax.ppermute(grad_rows, "aug", over_x)
    h_far_relay = lax.ppermute(cols(a ^ 3), "aug", over_x)
    _, (g_mine, h_mine) = lax.optimization_barrier((h_far_relay, (grad_rows, cols(a ^ 1))))
    g_near = lax.ppermute(g_mine, "aug", over_core)
    h_near = lax.ppermute(h_mine, "aug", over_core)
    g_relay = lax.ppermute(g_far, "aug", over_core)
    h_relay = lax.ppermute(h_far_relay, "aug", over_core)
    _, second = lax.optimization_barrier((h_far_relay, cols(a ^ 2)))
    h_far = lax.ppermute(second, "aug", over_x)
    return [
        (a * rows, cols(a), grad_rows),
        ((a ^ 1) * rows, h_near, g_near),
        ((a ^ 2) * rows, h_far, g_far),
        ((a ^ 3) * rows, h_relay, g_relay),
    ]


def butterfly_sum(value, n):
    if n == 4:
        got = {}
        for m in (1, 2, 3):
            got[m] = lax.ppermute(value, "aug", [(i, i ^ m) for i in range(4)])
        return (value + got[1]) + (got[2] + got[3])
    if n & (n - 1):
        return lax.psum(value, "aug")
    bit = 1
    while bit < n:
        value = value + lax.ppermute(value, "aug", [(i, i ^ bit) for i in range(n)])
        bit *= 2
    return value


def per_device(ring, hidden, output_grad, down_weight, first_moment, second_moment, noise):
    views = lax.axis_size("aug")
    groups = lax.axis_size("dp")
    images_here = hidden.shape[1]
    patches = hidden.shape[2]
    width = hidden.shape[3]
    model_width = output_grad.shape[3]
    images_all = images_here * groups
    clip = clip_ratio * math.sqrt(patches * width * model_width / views)
    local_rows = images_here * patches
    h_rows = hidden.reshape(local_rows, width)
    grad_rows = output_grad.reshape(local_rows, model_width)
    if views == 4 and images_here == 1:
        blocks = exchange_four(h_rows, grad_rows)
        slice_width = blocks[0][1].shape[1]
        summed = None
        for at, h_piece, g_piece in blocks:
            term = jnp.dot(h_piece.T, g_piece, preferred_element_type=jnp.float32)
            summed = term if summed is None else summed + term
        summed = summed[None]

        def project_all(step, after):
            if step < 1 or step > len(blocks):
                return None
            at, _, g_piece = blocks[step - 1]
            _, g_piece = lax.optimization_barrier((after, g_piece))
            return at, project_back(g_piece, down_weight).astype(jnp.bfloat16)

        hidden_grad = None
    else:
        swapped = lax.all_to_all(h_rows, "aug", split_axis=1, concat_axis=0, tiled=True)
        every = lax.all_gather(grad_rows, "aug", axis=0, tiled=True)
        slice_width = swapped.shape[1]
        h_four = swapped.reshape(views, images_here, patches, slice_width)
        g_four = every.reshape(views, images_here, patches, model_width)
        summed = jnp.einsum("vipf,vipd->ifd", h_four, g_four, preferred_element_type=jnp.float32)
        back_rows = project_back(every, down_weight)
        hidden_grad = back_rows.astype(jnp.bfloat16).reshape(views, images_here, patches, slice_width)
        project_all = None
    grads = summed / views
    partial_value = jnp.sum(grads * grads, axis=(1, 2))
    squares = butterfly_sum(partial_value, views)
    image_norms = jnp.sqrt(squares)
    factor = clip / jnp.maximum(image_norms, clip)
    owned_rows = slice_width // groups
    pieces = 4 if owned_rows % 32 == 0 else 2
    half = owned_rows // pieces

    def parts(block, which, after):
        source = grads
        if after is not None:
            _, source = lax.optimization_barrier((after, grads))
        start = block * owned_rows + which * half
        rows = lax.dynamic_slice_in_dim(source, start, half, axis=1)
        return lax.optimization_barrier(jnp.sum(factor[:, None, None] * rows, axis=0))

    owned, deferred = ring_reduce_scatter(parts, ring, pieces, project_all)
    if hidden_grad is None:
        out = jnp.zeros((views * local_rows, slice_width), jnp.bfloat16)
        items = [item for item in deferred if item is not None]
        for at, _, g_piece in blocks[len(items):]:
            items.append((at, project_back(g_piece, down_weight).astype(jnp.bfloat16)))
        for at, back in items:
            out = lax.dynamic_update_slice_in_dim(out, back, at, axis=0)
        hidden_grad = out.reshape(views, images_here, patches, slice_width)
    clipped_mean = owned / images_all
    noisy = clipped_mean + noise_ratio * clip * noise / images_all
    new_first = beta_one * first_moment + (1.0 - beta_one) * noisy
    new_second = beta_two * second_moment + (1.0 - beta_two) * noisy * noisy
    update = (
        new_first
        / (1.0 - beta_one**adam_step)
        / (jnp.sqrt(new_second / (1.0 - beta_two**adam_step)) + adam_eps)
    )
    return (image_norms, clipped_mean, new_first, new_second, update, hidden_grad)


def solution(mesh):
    in_specs = (
        P("aug", "dp", None, None),
        P("aug", "dp", None, None),
        P("aug", None),
        P(("aug", "dp"), None),
        P(("aug", "dp"), None),
        P(("aug", "dp"), None),
    )
    out_specs = (
        P("dp"),
        P(("aug", "dp"), None),
        P(("aug", "dp"), None),
        P(("aug", "dp"), None),
        P(("aug", "dp"), None),
        P(None, "dp", None, "aug"),
    )
    ring = ring_order(mesh)

    def body(*args):
        return per_device(ring, *args)

    return jax.shard_map(
        body, mesh=mesh, in_specs=in_specs, out_specs=out_specs, check_vma=False
    )
```

```python
import math

import jax
import jax.numpy as jnp
from jax import lax
from jax.sharding import PartitionSpec as P

clip_ratio = 1.9
noise_ratio = 0.002
beta_one = 0.9
beta_two = 0.999
adam_step = 10
adam_eps = 1e-08


def project_back(rows, down_weight):
    return lax.dot_general(
        rows, down_weight, (((1,), (1,)), ((), ())), preferred_element_type=jnp.float32
    )


def grid_cycle(points):
    zs = sorted({z for z, _ in points})
    ys = sorted({y for _, y in points})
    if len(zs) * len(ys) != len(points):
        return None
    swap = len(zs) % 2 == 1
    if swap:
        zs, ys = ys, zs
    rows, cols = len(zs), len(ys)
    if rows % 2 == 1 or cols < 2:
        return None
    walk = [(0, c) for c in range(cols)]
    for r in range(1, rows):
        order = range(cols - 1, 0, -1) if r % 2 == 1 else range(1, cols)
        walk += [(r, c) for c in order]
    walk += [(r, 0) for r in range(rows - 1, 0, -1)]
    cycle = [(zs[r], ys[c]) for r, c in walk]
    if swap:
        cycle = [(y, z) for z, y in cycle]
    return cycle


def ring_order(mesh):
    column = list(mesh.devices[0, :])
    n = len(column)
    try:
        places = [(int(d.coords[2]), int(d.coords[1])) for d in column]
    except Exception:
        return list(range(n))
    cycle = grid_cycle(places)
    if cycle is None or len(set(places)) != n:
        return list(range(n))
    return [places.index(p) for p in cycle]


def lookup(table, index):
    out = jnp.int32(table[0])
    for k in range(1, len(table)):
        out = jnp.where(index == k, jnp.int32(table[k]), out)
    return out


def ring_reduce_scatter(parts, ring, pieces, during=None):
    n = len(ring)
    pos_of = [0] * n
    for k, d in enumerate(ring):
        pos_of[d] = k
    me = lax.axis_index("dp")
    pos = lookup(pos_of, me)
    right = [(ring[k], ring[(k + 1) % n]) for k in range(n)]
    left = [(ring[k], ring[(k - 1) % n]) for k in range(n)]
    def block(s, step):
        return lookup(ring, (pos - 1 - s) % n if step < 0 else (pos + 1 + s) % n)

    chains = [(-1 if c % 2 == 0 else 1, c) for c in range(pieces)]
    own = [parts(block(0, step), which, None) for step, which in chains]
    extra = []
    acc = [None] * pieces
    for s in range(n - 1):
        send = [o if x is None else x + o for x, o in zip(acc, own)]
        if during is not None:
            extra.append(during(s, send))
        acc = [
            lax.ppermute(v, "dp", right if step < 0 else left)
            for v, (step, _) in zip(send, chains)
        ]
        own = [
            parts(block(s + 1, step), which, v)
            for v, (step, which) in zip(send, chains)
        ]
    return jnp.concatenate([x + o for x, o in zip(acc, own)], axis=0), extra


def exchange_four(h_rows, grad_rows):
    a = lax.axis_index("aug")
    rows = h_rows.shape[0]
    sw = h_rows.shape[1] // 4

    def cols(b):
        return lax.dynamic_slice_in_dim(h_rows, b * sw, sw, axis=1)

    over_x = [(i, i ^ 2) for i in range(4)]
    over_core = [(i, i ^ 1) for i in range(4)]
    g_far = lax.ppermute(grad_rows, "aug", over_x)
    h_far_relay = lax.ppermute(cols(a ^ 3), "aug", over_x)
    _, (g_mine, h_mine) = lax.optimization_barrier((h_far_relay, (grad_rows, cols(a ^ 1))))
    g_near = lax.ppermute(g_mine, "aug", over_core)
    h_near = lax.ppermute(h_mine, "aug", over_core)
    g_relay = lax.ppermute(g_far, "aug", over_core)
    h_relay = lax.ppermute(h_far_relay, "aug", over_core)
    _, second = lax.optimization_barrier((h_far_relay, cols(a ^ 2)))
    h_far = lax.ppermute(second, "aug", over_x)
    return [
        (a * rows, cols(a), grad_rows),
        ((a ^ 1) * rows, h_near, g_near),
        ((a ^ 2) * rows, h_far, g_far),
        ((a ^ 3) * rows, h_relay, g_relay),
    ]


def butterfly_sum(value, n):
    if n == 4:
        got = {}
        for m in (1, 2, 3):
            got[m] = lax.ppermute(value, "aug", [(i, i ^ m) for i in range(4)])
        return (value + got[1]) + (got[2] + got[3])
    if n & (n - 1):
        return lax.psum(value, "aug")
    bit = 1
    while bit < n:
        value = value + lax.ppermute(value, "aug", [(i, i ^ bit) for i in range(n)])
        bit *= 2
    return value


def per_device(ring, hidden, output_grad, down_weight, first_moment, second_moment, noise):
    views = lax.axis_size("aug")
    groups = lax.axis_size("dp")
    images_here = hidden.shape[1]
    patches = hidden.shape[2]
    width = hidden.shape[3]
    model_width = output_grad.shape[3]
    images_all = images_here * groups
    clip = clip_ratio * math.sqrt(patches * width * model_width / views)
    local_rows = images_here * patches
    h_rows = hidden.reshape(local_rows, width)
    grad_rows = output_grad.reshape(local_rows, model_width)
    if views == 4 and images_here == 1:
        blocks = exchange_four(h_rows, grad_rows)
        slice_width = blocks[0][1].shape[1]
        summed = None
        for at, h_piece, g_piece in blocks:
            term = jnp.dot(h_piece.T, g_piece, preferred_element_type=jnp.float32)
            summed = term if summed is None else summed + term
        summed = summed[None]

        def project_all(step, after):
            if step < 1 or step > len(blocks):
                return None
            at, _, g_piece = blocks[step - 1]
            _, g_piece = lax.optimization_barrier((after, g_piece))
            return at, project_back(g_piece, down_weight).astype(jnp.bfloat16)

        hidden_grad = None
    else:
        swapped = lax.all_to_all(h_rows, "aug", split_axis=1, concat_axis=0, tiled=True)
        every = lax.all_gather(grad_rows, "aug", axis=0, tiled=True)
        slice_width = swapped.shape[1]
        h_four = swapped.reshape(views, images_here, patches, slice_width)
        g_four = every.reshape(views, images_here, patches, model_width)
        summed = jnp.einsum("vipf,vipd->ifd", h_four, g_four, preferred_element_type=jnp.float32)
        back_rows = project_back(every, down_weight)
        hidden_grad = back_rows.astype(jnp.bfloat16).reshape(views, images_here, patches, slice_width)
        project_all = None
    grads = summed / views
    groups_of_rows = 10 if grads.shape[1] % 80 == 0 else 1
    per_group = jnp.sum(
        (grads * grads).reshape(grads.shape[0], groups_of_rows, -1, grads.shape[2]),
        axis=(2, 3),
    )
    partial_value = jnp.sum(lax.optimization_barrier(per_group), axis=1)
    squares = butterfly_sum(partial_value, views)
    image_norms = jnp.sqrt(squares)
    factor = clip / jnp.maximum(image_norms, clip)
    owned_rows = slice_width // groups
    pieces = 4 if owned_rows % 32 == 0 else 2
    half = owned_rows // pieces

    def parts(block, which, after):
        source = grads
        if after is not None:
            _, source = lax.optimization_barrier((after, grads))
        start = block * owned_rows + which * half
        rows = lax.dynamic_slice_in_dim(source, start, half, axis=1)
        return lax.optimization_barrier(jnp.sum(factor[:, None, None] * rows, axis=0))

    owned, deferred = ring_reduce_scatter(parts, ring, pieces, project_all)
    if hidden_grad is None:
        out = jnp.zeros((views * local_rows, slice_width), jnp.bfloat16)
        items = [item for item in deferred if item is not None]
        for at, _, g_piece in blocks[len(items):]:
            items.append((at, project_back(g_piece, down_weight).astype(jnp.bfloat16)))
        for at, back in items:
            out = lax.dynamic_update_slice_in_dim(out, back, at, axis=0)
        hidden_grad = out.reshape(views, images_here, patches, slice_width)
    clipped_mean = owned / images_all
    noisy = clipped_mean + noise_ratio * clip * noise / images_all
    new_first = beta_one * first_moment + (1.0 - beta_one) * noisy
    new_second = beta_two * second_moment + (1.0 - beta_two) * noisy * noisy
    update = (
        new_first
        / (1.0 - beta_one**adam_step)
        / (jnp.sqrt(new_second / (1.0 - beta_two**adam_step)) + adam_eps)
    )
    return (image_norms, clipped_mean, new_first, new_second, update, hidden_grad)


def solution(mesh):
    in_specs = (
        P("aug", "dp", None, None),
        P("aug", "dp", None, None),
        P("aug", None),
        P(("aug", "dp"), None),
        P(("aug", "dp"), None),
        P(("aug", "dp"), None),
    )
    out_specs = (
        P("dp"),
        P(("aug", "dp"), None),
        P(("aug", "dp"), None),
        P(("aug", "dp"), None),
        P(("aug", "dp"), None),
        P(None, "dp", None, "aug"),
    )
    ring = ring_order(mesh)

    def body(*args):
        return per_device(ring, *args)

    return jax.shard_map(
        body, mesh=mesh, in_specs=in_specs, out_specs=out_specs, check_vma=False
    )
```
